512 devices in a mesh: sec: 2 (over core), atoms: 32 (over z_lo, y), batch: 8 (over z_hi, x).
Axes of the slice: x: 4, y: 8, z: 8 (z_hi: 2, z_lo: 4; z = z_hi * 4 + z_lo), core: 2. Of those that a mesh axis runs over, the one named last changes fastest.
Arguments:
- atoms_in: bfloat16 [8, 16384, 1024], P('batch', 'atoms', 'sec'), may hold values from -6 to 6
- tile_ids: int32 [8, 2, 512], P('batch', None, 'atoms'), may hold values from -1 to 127, as said below
- tile_vals: bfloat16 [8, 512, 128, 128], P('batch', 'atoms'), may hold values from -0.26367188 to 0.26367188
- seq_lens: int32 [8], P('batch'), may hold values from 8193 to 16384, as said below
- pair_labels: int32 [8, 16384], P('batch', 'atoms'), may hold values from 0 to 255
- peak_embed: bfloat16 [8, 256, 256], P('batch', 'sec'), may hold values from -6 to 6
- norm_gain: bfloat16 [1024], P('sec'), may hold values from 0.099609375 to 1.8984375
- w_query: bfloat16 [1024, 512], P(None, 'sec'), may hold values from -0.1875 to 0.1875
- w_key: bfloat16 [1024, 512], P(None, 'sec'), may hold values from -0.1875 to 0.1875
- w_value: bfloat16 [1024, 512], P(None, 'sec'), may hold values from -0.1875 to 0.1875
- w_out: bfloat16 [512, 1024], P('sec'), may hold values from -0.25 to 0.25
- w_proj: bfloat16 [1024, 256], P('sec'), may hold values from -0.1875 to 0.1875
Outputs:
- hidden_two: bfloat16 [8, 16384, 1024], P('batch', 'atoms', 'sec')
- seq_loss: float32 [8], P('batch')
- proj_grad: float32 [8, 1024, 256], P('batch', 'sec')
The draws below stay inside these ranges and needn't reach their ends.
Inputs may be any that keep to these rules, and one draw needn't show every extreme that they name: `tile_ids`: each index of atoms owns 16 consecutive slots and the row blocks 4 i to 4 (i + 1) - 1; its first 4 slots hold the diagonal tiles of its row blocks; live slots come first and padded slots have both ids -1; every live tile's row block is one of its owner's and its column block lies within 2 blocks of it; in every sequence some index of atoms has all 16 slots live. `seq_lens`: at least one sequence has all 16384 atoms live.
All inputs are finite; a program needn't handle non-finite values.
Results may differ from the reference program's by a relative error of at most 0.013.
Values may be sent and summed in bfloat16 or wider, within the bound.
No kernel may reach another device: no remote copies, remote signals or barrier semaphores. Data moves between devices by JAX's collectives and lax.ppermute only.
A program may use at most 64 MiB of HBM per device.

```python
import math
import jax
import jax.numpy as jnp
from jax import lax

D = 1024
HEADS = 8
HEAD_DIM = 64
EMBED = 256
PEAKS = 256
TILE = 128
TILES_PER_BLOCK = 4
TOK_DEV = 512
SEQS = 8
ATOMS = 16384
BLOCKS_DEV = 4
REACH = 2
SLOTS = 16
TILES = 512


def draw_tile_ids(key, part):
    shard_count = ATOMS // TOK_DEV
    block_total = ATOMS // TILE
    keys_all = jax.random.split(key, 5)
    least_count = BLOCKS_DEV + 2 + (SLOTS - BLOCKS_DEV - 2) // 4
    counts = jax.random.randint(keys_all[0], (SEQS, shard_count), least_count, SLOTS + 1)
    fullest = jax.random.randint(keys_all[1], (SEQS, 1), 0, shard_count)
    shard_ids = jnp.arange(shard_count, dtype=jnp.int32)[None, :]
    counts = jnp.where(shard_ids == fullest, SLOTS, counts)
    slot_ids = jnp.arange(SLOTS, dtype=jnp.int32)[None, None, :]
    first_block = (shard_ids * BLOCKS_DEV)[:, :, None]
    local_pick = jax.random.randint(keys_all[2], (SEQS, shard_count, SLOTS), 0, BLOCKS_DEV)
    distance = jax.random.randint(keys_all[3], (SEQS, shard_count, SLOTS), 1, REACH + 1)
    direction = 2 * jax.random.randint(keys_all[4], (SEQS, shard_count, SLOTS), 0, 2) - 1
    row_local = jnp.where(slot_ids < BLOCKS_DEV, slot_ids, local_pick)
    row_local = jnp.where(slot_ids == BLOCKS_DEV, BLOCKS_DEV - 1, row_local)
    row_local = jnp.where(slot_ids == BLOCKS_DEV + 1, 0, row_local)
    offset = jnp.where(slot_ids < BLOCKS_DEV, 0, direction * distance)
    offset = jnp.where(slot_ids == BLOCKS_DEV, REACH, offset)
    offset = jnp.where(slot_ids == BLOCKS_DEV + 1, -REACH, offset)
    row_global = first_block + row_local
    col_global = jnp.clip(row_global + offset, 0, block_total - 1)
    live_slots = slot_ids < counts[:, :, None]
    row_final = jnp.where(live_slots, row_global, -1).reshape(SEQS, TILES)
    col_final = jnp.where(live_slots, col_global, -1).reshape(SEQS, TILES)
    return jnp.stack([row_final, col_final], axis=1).astype(jnp.int32)


def draw_seq_lens(key, part):
    keys_all = jax.random.split(key, 2)
    lengths = ATOMS - jax.random.randint(keys_all[0], (SEQS,), 0, ATOMS // 2)
    fullest = jax.random.randint(keys_all[1], (), 0, SEQS)
    return jnp.where(jnp.arange(SEQS, dtype=jnp.int32) == fullest, ATOMS, lengths).astype(jnp.int32)


def place_ends(values, key, smallest, high):
    index_at = [jax.random.randint(jax.random.fold_in(key, axis), (), 0, length) for axis, length in enumerate(values.shape)]
    longest = values.shape.index(max(values.shape))
    neighbour = index_at[:longest] + [(index_at[longest] + 1) % values.shape[longest]] + index_at[longest + 1:]
    return values.at[tuple(index_at)].set(smallest).at[tuple(neighbour)].set(high)


def levels(key, extent, cuts, smallest, high):
    def one(dim, blocks):
        steps = jax.random.uniform(jax.random.fold_in(jax.random.fold_in(key, 6), dim), (blocks,), jnp.float32, smallest / len(cuts), high / len(cuts))
        return jnp.repeat(jnp.exp(steps), extent[dim] // blocks).reshape((-1,) + (1,) * (len(extent) - dim - 1))

    level = one(*cuts[0])
    for cut in cuts[1:]:
        level = level * one(*cut)
    return level


def bell_draw(rng, extent, width, bound, cuts=(), kind=jnp.bfloat16):
    entries = width * jax.random.normal(rng, extent, jnp.float32)
    if cuts:
        entries = entries * levels(rng, extent, cuts, -0.22, 0.18)
    return jnp.clip(entries, -bound, bound).astype(kind)


def setup_inputs(seed: int = 0) -> dict:
    arg_keys = jax.random.split(jax.random.key(seed), 13)
    atoms_in = bell_draw(arg_keys[0], (SEQS, ATOMS, D), 1.0, 6.0, ((0, 8), (1, 32), (2, 2)))
    tile_ids = draw_tile_ids(jax.random.fold_in(arg_keys[12], 71), 0)
    tile_vals = bell_draw(arg_keys[2], (SEQS, TILES, TILE, TILE), ((TILES_PER_BLOCK * TILE) ** -0.5), 0.26367188, ((0, 8), (1, 32)))
    seq_lens = draw_seq_lens(jax.random.fold_in(arg_keys[12], 71), 0)
    pair_labels = place_ends(jax.random.randint(arg_keys[4], (SEQS, ATOMS), 0, PEAKS), jax.random.fold_in(arg_keys[4], 1), 0, PEAKS - 1).astype(jnp.int32)
    peak_embed = bell_draw(arg_keys[5], (SEQS, PEAKS, EMBED), 1.0, 6.0, ((0, 8), (1, 2)))
    norm_gain = jnp.clip(1.0 + 0.18 * jax.random.normal(arg_keys[6], (D,), jnp.float32), 0.099609375, 1.8984375).astype(jnp.bfloat16)
    w_query = bell_draw(arg_keys[7], (D, HEADS * HEAD_DIM), D ** -0.5, 0.1875, ((1, 2),))
    w_key = bell_draw(arg_keys[8], (D, HEADS * HEAD_DIM), D ** -0.5, 0.1875, ((1, 2),))
    w_value = bell_draw(arg_keys[9], (D, HEADS * HEAD_DIM), D ** -0.5, 0.1875, ((1, 2),))
    w_out = bell_draw(arg_keys[10], (HEADS * HEAD_DIM, D), (HEADS * HEAD_DIM) ** -0.5, 0.25, ((0, 2),))
    w_proj = bell_draw(arg_keys[11], (D, EMBED), D ** -0.5, 0.1875, ((0, 2),))
    return dict(atoms_in=atoms_in, tile_ids=tile_ids, tile_vals=tile_vals, seq_lens=seq_lens, pair_labels=pair_labels, peak_embed=peak_embed, norm_gain=norm_gain, w_query=w_query, w_key=w_key, w_value=w_value, w_out=w_out, w_proj=w_proj)


EPSILON = 1e-06
HIGHEST = lax.Precision.HIGHEST

def feature_map(values):
    return jax.nn.elu(values) + 1.0

def reference(atoms_in, tile_ids, tile_vals, seq_lens, pair_labels, peak_embed, norm_gain, w_query, w_key, w_value, w_out, w_proj):
    block_count = ATOMS // TILE
    inner_width = HEADS * HEAD_DIM
    logit_scale = 2.0 / math.sqrt(EMBED)
    slope_scale = 1.0 / math.sqrt(PEAKS)

    def one_sequence(packed):
        atom_rows, tile_pair, tile_block, length_one, label_row, peak_rows = packed
        row_ids = tile_pair[0]
        col_ids = tile_pair[1]
        live_mask = (row_ids >= 0).astype(jnp.float32)
        blocks = atom_rows.reshape(block_count, TILE, D)
        panels = jnp.take(blocks, jnp.clip(col_ids, 0, block_count - 1).astype(jnp.int32), axis=0)
        products = jnp.einsum('tij,tjf->tif', tile_block.astype(jnp.float32), panels.astype(jnp.float32), precision=HIGHEST)
        products = products * live_mask[:, None, None]
        summed = jax.ops.segment_sum(products, jnp.clip(row_ids, 0, block_count - 1).astype(jnp.int32), num_segments=block_count)
        gathered = summed.reshape(ATOMS, D).astype(jnp.bfloat16)
        hidden_one = (atom_rows.astype(jnp.float32) + gathered.astype(jnp.float32)).astype(jnp.bfloat16)
        hidden_f = hidden_one.astype(jnp.float32)
        row_scale = lax.rsqrt(lax.optimization_barrier(jnp.mean(hidden_f * hidden_f, axis=-1, keepdims=True)) + EPSILON)
        normed = (hidden_f * row_scale * norm_gain.astype(jnp.float32)).astype(jnp.bfloat16)
        queries = jnp.dot(normed, w_query, preferred_element_type=jnp.float32).astype(jnp.bfloat16)
        key_rows = jnp.dot(normed, w_key, preferred_element_type=jnp.float32).astype(jnp.bfloat16)
        value_rows = jnp.dot(normed, w_value, preferred_element_type=jnp.float32).astype(jnp.bfloat16)
        atom_mask = (jnp.arange(ATOMS, dtype=jnp.int32) < length_one).astype(jnp.float32)
        feat_query = feature_map(queries.astype(jnp.float32)).reshape(ATOMS, HEADS, HEAD_DIM)
        feat_keys = feature_map(key_rows.astype(jnp.float32)).reshape(ATOMS, HEADS, HEAD_DIM) * atom_mask[:, None, None]
        value_f = value_rows.astype(jnp.float32).reshape(ATOMS, HEADS, HEAD_DIM)
        outer_state = jnp.einsum('nhd,nhe->hde', feat_keys, value_f, precision=HIGHEST)
        key_total = lax.optimization_barrier(jnp.sum(feat_keys, axis=0))
        numerator = jnp.einsum('nhd,hde->nhe', feat_query, outer_state, precision=HIGHEST)
        denominator = jnp.einsum('nhd,hd->nh', feat_query, key_total, precision=HIGHEST)
        attended = (numerator / denominator[..., None]).reshape(ATOMS, inner_width)
        out_scale = lax.rsqrt(lax.optimization_barrier(jnp.mean(attended * attended, axis=-1, keepdims=True)) + EPSILON)
        attended_n = (attended * out_scale).astype(jnp.bfloat16)
        branch = jnp.dot(attended_n, w_out, preferred_element_type=jnp.float32)
        hidden_two = (hidden_f + branch).astype(jnp.bfloat16)
        embedded = jnp.dot(hidden_two, w_proj, preferred_element_type=jnp.float32)
        embed_scale = lax.rsqrt(lax.optimization_barrier(jnp.mean(embedded * embedded, axis=-1, keepdims=True)) + EPSILON)
        unit_rows = embedded * embed_scale
        peak_f = peak_rows.astype(jnp.float32)
        logits = logit_scale * jnp.dot(unit_rows, peak_f.T, precision=HIGHEST)
        target = (label_row[:, None] == jnp.arange(PEAKS, dtype=jnp.int32)[None, :]).astype(jnp.float32)
        sign_rows = 2.0 * target - 1.0
        per_atom = lax.optimization_barrier(jnp.mean(jax.nn.softplus(-sign_rows * logits), axis=-1))
        loss_one = jnp.sum(per_atom * atom_mask) / ATOMS
        slopes = atom_mask[:, None] * (jax.nn.sigmoid(logits) - target) * slope_scale
        unit_grad = logit_scale * jnp.dot(slopes, peak_f, precision=HIGHEST)
        embed_grad = (embed_scale * (unit_grad - unit_rows * lax.optimization_barrier(jnp.mean(unit_grad * unit_rows, axis=-1, keepdims=True)))).astype(jnp.bfloat16)
        grad_one = jnp.einsum('nd,ne->de', hidden_two, embed_grad, preferred_element_type=jnp.float32)
        return (hidden_two, loss_one, grad_one)
    hidden_all, losses, grads = lax.map(one_sequence, (atoms_in, tile_ids, tile_vals, seq_lens, pair_labels, peak_embed))
    return (hidden_all, losses, grads)
```

```python
import math

import jax
import jax.numpy as jnp
from jax import lax
from jax.sharding import PartitionSpec as P

D = 1024
HEADS = 8
HEAD_DIM = 64
PEAKS = 256


EPSILON = 1e-06
HIGHEST = lax.Precision.HIGHEST


def extended(x, sides, width):
    for axis, dim in sides:
        peers, length = (lax.axis_size(axis), x.shape[dim])
        up = [(i, (i + 1) % peers) for i in range(peers - 1)]
        down = [(j, i) for i, j in up]
        last = lax.slice_in_dim(x, length - width, length, axis=dim)
        leading = lax.slice_in_dim(x, 0, width, axis=dim)
        before = lax.ppermute(last, axis, up)
        after = lax.ppermute(leading, axis, down)
        x = jnp.concatenate([before, x, after], axis=dim)
    return x


def swap_sec(x):
    return lax.ppermute(x, "sec", [(0, 1), (1, 0)])


def sum_sec(x):
    return x + swap_sec(x)


def sum_atoms(x):
    peers = lax.axis_size("atoms")
    if peers & (peers - 1):
        return lax.psum(x, "atoms")
    stride = 1
    while stride < peers:
        pairs = [(i, i ^ stride) for i in range(peers)]
        x = x + lax.ppermute(x, "atoms", pairs)
        stride *= 2
    return x


def feature_map(values):
    return jax.nn.elu(values) + 1.0


def message_pass(atom_rows, tile_pair, tile_block):
    tile_size = tile_block.shape[-1]
    local_rows, half_width = atom_rows.shape
    block_count = local_rows // tile_size
    reach_blocks = max(block_count // 2, 1)
    padded = extended(atom_rows, (("atoms", 0),), reach_blocks * tile_size)
    blocks = padded.reshape(block_count + 2 * reach_blocks, tile_size, half_width)
    first_block = lax.axis_index("atoms") * block_count
    row_ids = tile_pair[0]
    col_ids = tile_pair[1]
    live_tiles = row_ids >= 0
    col_local = jnp.where(live_tiles, col_ids - first_block + reach_blocks, 0)
    row_local = jnp.where(live_tiles, row_ids - first_block, -1)
    panels = jnp.take(blocks, col_local, axis=0)
    products = jnp.einsum("tij,tjf->tif", tile_block, panels, preferred_element_type=jnp.float32)
    selector = (row_local[None, :] == jnp.arange(block_count, dtype=jnp.int32)[:, None]).astype(
        jnp.float32
    )
    summed = jnp.einsum("bt,tif->bif", selector, products, precision=HIGHEST)
    return summed.reshape(local_rows, half_width).astype(jnp.bfloat16)


def key_summary(key_rows, value_rows, atom_mask, head_count):
    count_rows = key_rows.shape[0]
    feat_keys = (
        feature_map(key_rows.astype(jnp.float32)).reshape(count_rows, head_count, -1)
        * atom_mask[:, None, None]
    )
    value_f = value_rows.astype(jnp.float32).reshape(count_rows, head_count, -1)
    outer_state = jnp.einsum("nhd,nhe->hde", feat_keys, value_f, precision=HIGHEST)
    return (outer_state, jnp.sum(feat_keys, axis=0))


def read_summary(query_rows, outer_state, key_total, head_count):
    count_rows = query_rows.shape[0]
    feat_query = feature_map(query_rows.astype(jnp.float32)).reshape(count_rows, head_count, -1)
    numerator = jnp.einsum("nhd,hde->nhe", feat_query, outer_state, precision=HIGHEST)
    denominator = jnp.einsum("nhd,hd->nh", feat_query, key_total, precision=HIGHEST)
    return (numerator / denominator[..., None]).reshape(count_rows, -1)


def contrast(unit_rows, peak_rows, label_part, mask_part, peak_start):
    logit_scale = 2.0 / math.sqrt(unit_rows.shape[-1])
    peak_f = peak_rows.astype(jnp.float32)
    logits = logit_scale * jnp.dot(unit_rows, peak_f.T, precision=HIGHEST)
    peak_index = peak_start + jnp.arange(peak_rows.shape[0], dtype=jnp.int32)
    target = (label_part[:, None] == peak_index[None, :]).astype(jnp.float32)
    sign_rows = 2.0 * target - 1.0
    loss_part = jnp.sum(mask_part[:, None] * jax.nn.softplus(-sign_rows * logits)) / PEAKS
    slopes = mask_part[:, None] * (jax.nn.sigmoid(logits) - target) * (1.0 / math.sqrt(PEAKS))
    unit_grad = logit_scale * jnp.dot(slopes, peak_f, precision=HIGHEST)
    return (loss_part, unit_grad)


def embed_backward(unit_rows, unit_grad, embed_scale):
    inner_mean = jnp.mean(unit_grad * unit_rows, axis=-1, keepdims=True)
    return (embed_scale * (unit_grad - unit_rows * inner_mean)).astype(jnp.bfloat16)


def shards(
    atoms_in,
    tile_ids,
    tile_vals,
    seq_lens,
    pair_labels,
    peak_embed,
    norm_gain,
    w_query,
    w_key,
    w_value,
    w_out,
    w_proj,
):
    atom_rows = atoms_in[0]
    local_rows = atom_rows.shape[0]
    gathered = message_pass(atom_rows, tile_ids[0], tile_vals[0])
    hidden_one = (atom_rows.astype(jnp.float32) + gathered.astype(jnp.float32)).astype(jnp.bfloat16)
    atom_base = lax.axis_index("atoms") * local_rows
    length_one = seq_lens[0]
    label_row = pair_labels[0]
    peak_part = peak_embed[0]
    hidden_f = hidden_one.astype(jnp.float32)
    square_sum = lax.psum(jnp.sum(hidden_f * hidden_f, axis=-1), "sec")
    row_scale = lax.rsqrt(square_sum[:, None] / D + EPSILON)
    normed = (hidden_f * row_scale * norm_gain.astype(jnp.float32)).astype(jnp.bfloat16)
    head_cols = w_query.shape[1]
    sec = lax.axis_index("sec")
    width = normed.shape[1]
    other_rows = swap_sec(normed)

    def project(weight):
        halves = weight.reshape(2, width, weight.shape[1])
        mine = jnp.dot(normed, halves[sec], preferred_element_type=jnp.float32)
        return mine + jnp.dot(other_rows, halves[1 - sec], preferred_element_type=jnp.float32)

    query_f, key_f, value_f = tuple((project(weight) for weight in (w_query, w_key, w_value)))
    head_count = head_cols // HEAD_DIM
    atom_mask = (atom_base + jnp.arange(local_rows, dtype=jnp.int32) < length_one).astype(
        jnp.float32
    )
    outer_state, key_total = key_summary(
        key_f.astype(jnp.bfloat16), value_f.astype(jnp.bfloat16), atom_mask, head_count
    )
    packed = sum_atoms(jnp.concatenate([outer_state, key_total[:, None, :]], axis=1))
    outer_state, key_total = packed[:, :HEAD_DIM, :], packed[:, HEAD_DIM, :]
    attended = read_summary(query_f.astype(jnp.bfloat16), outer_state, key_total, head_count)
    out_sum = lax.psum(jnp.sum(attended * attended, axis=-1), "sec")
    attended_n = (attended * lax.rsqrt(out_sum[:, None] / (HEADS * HEAD_DIM) + EPSILON)).astype(
        jnp.bfloat16
    )
    out_cols = w_out.reshape(w_out.shape[0], 2, width)
    sent = jnp.dot(attended_n, out_cols[:, 1 - sec, :], preferred_element_type=jnp.float32)
    kept = jnp.dot(attended_n, out_cols[:, sec, :], preferred_element_type=jnp.float32)
    branch = kept + swap_sec(sent)
    hidden_two = (hidden_f + branch).astype(jnp.bfloat16)
    embedded = sum_sec(jnp.dot(hidden_two, w_proj, preferred_element_type=jnp.float32))
    embed_scale = lax.rsqrt(jnp.mean(embedded * embedded, axis=-1, keepdims=True) + EPSILON)
    unit_rows = embedded * embed_scale
    peak_start = sec * peak_part.shape[0]
    loss_part, unit_grad = contrast(unit_rows, peak_part, label_row, atom_mask, peak_start)
    unit_grad = sum_sec(unit_grad)
    embed_grad = embed_backward(unit_rows, unit_grad, embed_scale)
    proj_part = jnp.einsum("nd,ne->de", hidden_two, embed_grad, preferred_element_type=jnp.float32)
    loss_pair = sum_sec(loss_part)
    loss_rows = jnp.zeros((8, proj_part.shape[1]), jnp.float32).at[0, 0].set(loss_pair)
    packed = sum_atoms(jnp.concatenate([proj_part, loss_rows], axis=0))
    proj_total = packed[: proj_part.shape[0]]
    loss_total = packed[proj_part.shape[0], 0] / (local_rows * lax.axis_size("atoms"))
    return (hidden_two[None], loss_total.reshape(1), proj_total[None])


def solution(mesh):
    return jax.shard_map(
        shards,
        mesh=mesh,
        in_specs=(
            P("batch", "atoms", "sec"),
            P("batch", None, "atoms"),
            P("batch", "atoms", None, None),
            P("batch"),
            P("batch", "atoms"),
            P("batch", "sec", None),
            P("sec"),
            P(None, "sec"),
            P(None, "sec"),
            P(None, "sec"),
            P("sec", None),
            P("sec", None),
        ),
        out_specs=(P("batch", "atoms", "sec"), P("batch"), P("batch", "sec", None)),
        check_vma=False,
    )
```

```python
import math

import jax
import jax.numpy as jnp
from jax import lax
from jax.sharding import PartitionSpec as P

D = 1024
HEADS = 8
HEAD_DIM = 64
PEAKS = 256


EPSILON = 1e-06
HIGHEST = lax.Precision.HIGHEST


def extended(x, sides, width):
    for axis, dim in sides:
        peers, length = (lax.axis_size(axis), x.shape[dim])
        up = [(i, (i + 1) % peers) for i in range(peers - 1)]
        down = [(j, i) for i, j in up]
        last = lax.slice_in_dim(x, length - width, length, axis=dim)
        leading = lax.slice_in_dim(x, 0, width, axis=dim)
        before = lax.ppermute(last, axis, up)
        after = lax.ppermute(leading, axis, down)
        x = jnp.concatenate([before, x, after], axis=dim)
    return x


def swap_sec(x):
    return lax.ppermute(x, "sec", [(0, 1), (1, 0)])


def sum_sec(x):
    return x + swap_sec(x)


def butterfly(x, strides):
    peers = lax.axis_size("atoms")
    for stride in strides:
        pairs = [(i, i ^ stride) for i in range(peers)]
        x = x + lax.ppermute(x, "atoms", pairs)
    return x


def sum_atoms(x):
    peers = lax.axis_size("atoms")
    if peers & (peers - 1):
        return lax.psum(x, "atoms")
    inner = min(peers, 8)
    low = [1 << k for k in range(inner.bit_length() - 1)]
    high = [inner << k for k in range((peers // inner).bit_length() - 1)]
    half = (x.shape[0] // 2 + 7) // 8 * 8
    first = butterfly(x[:half], low + high)
    second = butterfly(x[half:], high + low)
    return jnp.concatenate([first, second], axis=0)


def feature_map(values):
    return jax.nn.elu(values) + 1.0


def message_pass(atom_rows, tile_pair, tile_block):
    tile_size = tile_block.shape[-1]
    local_rows, half_width = atom_rows.shape
    block_count = local_rows // tile_size
    reach_blocks = max(block_count // 2, 1)
    padded = extended(atom_rows, (("atoms", 0),), reach_blocks * tile_size)
    blocks = padded.reshape(block_count + 2 * reach_blocks, tile_size, half_width)
    first_block = lax.axis_index("atoms") * block_count
    row_ids = tile_pair[0]
    col_ids = tile_pair[1]
    live_tiles = row_ids >= 0
    col_local = jnp.where(live_tiles, col_ids - first_block + reach_blocks, 0)
    row_local = jnp.where(live_tiles, row_ids - first_block, -1)
    panels = jnp.take(blocks, col_local, axis=0)
    selector = row_local[None, :] == jnp.arange(block_count, dtype=jnp.int32)[:, None]
    masked = jnp.where(selector[:, :, None, None], tile_block[None], jnp.zeros_like(tile_block[None]))
    summed = jnp.einsum("btij,tjf->bif", masked, panels, preferred_element_type=jnp.float32)
    return summed.reshape(local_rows, half_width).astype(jnp.bfloat16)


def key_summary(key_rows, value_rows, atom_mask, head_count):
    count_rows = key_rows.shape[0]
    feat_keys = (
        feature_map(key_rows.astype(jnp.float32)).reshape(count_rows, head_count, -1)
        * atom_mask[:, None, None]
    )
    value_f = value_rows.astype(jnp.float32).reshape(count_rows, head_count, -1)
    outer_state = jnp.einsum("nhd,nhe->hde", feat_keys, value_f, precision=HIGHEST)
    return (outer_state, jnp.sum(feat_keys, axis=0))


def read_summary(query_rows, outer_state, key_total, head_count):
    count_rows = query_rows.shape[0]
    feat_query = feature_map(query_rows.astype(jnp.float32)).reshape(count_rows, head_count, -1)
    numerator = jnp.einsum("nhd,hde->nhe", feat_query, outer_state, precision=HIGHEST)
    denominator = jnp.einsum("nhd,hd->nh", feat_query, key_total, precision=HIGHEST)
    return (numerator / denominator[..., None]).reshape(count_rows, -1)


def contrast(unit_rows, peak_rows, label_part, mask_part, peak_start):
    logit_scale = 2.0 / math.sqrt(unit_rows.shape[-1])
    peak_f = peak_rows.astype(jnp.float32)
    logits = logit_scale * jnp.dot(unit_rows, peak_f.T, precision=HIGHEST)
    peak_index = peak_start + jnp.arange(peak_rows.shape[0], dtype=jnp.int32)
    target = (label_part[:, None] == peak_index[None, :]).astype(jnp.float32)
    sign_rows = 2.0 * target - 1.0
    loss_part = jnp.sum(mask_part[:, None] * jax.nn.softplus(-sign_rows * logits)) / PEAKS
    slopes = mask_part[:, None] * (jax.nn.sigmoid(logits) - target) * (1.0 / math.sqrt(PEAKS))
    unit_grad = logit_scale * jnp.dot(slopes, peak_f, precision=HIGHEST)
    return (loss_part, unit_grad)


def embed_backward(unit_rows, unit_grad, embed_scale):
    inner_mean = jnp.mean(unit_grad * unit_rows, axis=-1, keepdims=True)
    return (embed_scale * (unit_grad - unit_rows * inner_mean)).astype(jnp.bfloat16)


def shards(
    atoms_in,
    tile_ids,
    tile_vals,
    seq_lens,
    pair_labels,
    peak_embed,
    norm_gain,
    w_query,
    w_key,
    w_value,
    w_out,
    w_proj,
):
    atom_rows = atoms_in[0]
    local_rows = atom_rows.shape[0]
    gathered = message_pass(atom_rows, tile_ids[0], tile_vals[0])
    hidden_one = (atom_rows.astype(jnp.float32) + gathered.astype(jnp.float32)).astype(jnp.bfloat16)
    atom_base = lax.axis_index("atoms") * local_rows
    length_one = seq_lens[0]
    label_row = pair_labels[0]
    peak_part = peak_embed[0]
    hidden_f = hidden_one.astype(jnp.float32)
    square_sum = lax.psum(jnp.sum(hidden_f * hidden_f, axis=-1), "sec")
    row_scale = lax.rsqrt(square_sum[:, None] / D + EPSILON)
    normed = (hidden_f * row_scale * norm_gain.astype(jnp.float32)).astype(jnp.bfloat16)
    head_cols = w_query.shape[1]
    sec = lax.axis_index("sec")
    width = normed.shape[1]
    other_rows = swap_sec(normed)

    def project(weight):
        halves = weight.reshape(2, width, weight.shape[1])
        mine = jnp.dot(normed, halves[sec], preferred_element_type=jnp.float32)
        return mine + jnp.dot(other_rows, halves[1 - sec], preferred_element_type=jnp.float32)

    query_f, key_f, value_f = tuple((project(weight) for weight in (w_query, w_key, w_value)))
    head_count = head_cols // HEAD_DIM
    atom_mask = (atom_base + jnp.arange(local_rows, dtype=jnp.int32) < length_one).astype(
        jnp.float32
    )
    outer_state, key_total = key_summary(
        key_f.astype(jnp.bfloat16), value_f.astype(jnp.bfloat16), atom_mask, head_count
    )
    state_rows = jnp.concatenate([outer_state, key_total[:, None, :]], axis=1)
    packed = sum_atoms(state_rows.reshape(-1, HEAD_DIM)).reshape(state_rows.shape)
    outer_state, key_total = packed[:, :HEAD_DIM, :], packed[:, HEAD_DIM, :]
    attended = read_summary(query_f.astype(jnp.bfloat16), outer_state, key_total, head_count)
    out_sum = lax.psum(jnp.sum(attended * attended, axis=-1), "sec")
    attended_n = (attended * lax.rsqrt(out_sum[:, None] / (HEADS * HEAD_DIM) + EPSILON)).astype(
        jnp.bfloat16
    )
    out_cols = w_out.reshape(w_out.shape[0], 2, width)
    sent = jnp.dot(attended_n, out_cols[:, 1 - sec, :], preferred_element_type=jnp.float32)
    kept = jnp.dot(attended_n, out_cols[:, sec, :], preferred_element_type=jnp.float32)
    branch = kept + swap_sec(sent)
    hidden_two = (hidden_f + branch).astype(jnp.bfloat16)
    embedded = sum_sec(jnp.dot(hidden_two, w_proj, preferred_element_type=jnp.float32))
    embed_scale = lax.rsqrt(jnp.mean(embedded * embedded, axis=-1, keepdims=True) + EPSILON)
    unit_rows = embedded * embed_scale
    peak_start = sec * peak_part.shape[0]
    loss_part, unit_grad = contrast(unit_rows, peak_part, label_row, atom_mask, peak_start)
    unit_grad = sum_sec(unit_grad)
    embed_grad = embed_backward(unit_rows, unit_grad, embed_scale)
    proj_part = jnp.einsum("nd,ne->de", hidden_two, embed_grad, preferred_element_type=jnp.float32)
    loss_pair = sum_sec(loss_part)
    loss_rows = jnp.zeros((8, proj_part.shape[1]), jnp.float32).at[0, 0].set(loss_pair)
    packed = sum_atoms(jnp.concatenate([proj_part, loss_rows], axis=0))
    proj_total = packed[: proj_part.shape[0]]
    loss_total = packed[proj_part.shape[0], 0] / (local_rows * lax.axis_size("atoms"))
    return (hidden_two[None], loss_total.reshape(1), proj_total[None])


def solution(mesh):
    return jax.shard_map(
        shards,
        mesh=mesh,
        in_specs=(
            P("batch", "atoms", "sec"),
            P("batch", None, "atoms"),
            P("batch", "atoms", None, None),
            P("batch"),
            P("batch", "atoms"),
            P("batch", "sec", None),
            P("sec"),
            P(None, "sec"),
            P(None, "sec"),
            P(None, "sec"),
            P("sec", None),
            P("sec", None),
        ),
        out_specs=(P("batch", "atoms", "sec"), P("batch"), P("batch", "sec", None)),
        check_vma=False,
    )
```

```python
import math

import jax
import jax.numpy as jnp
from jax import lax
from jax.sharding import PartitionSpec as P

D = 1024
HEADS = 8
HEAD_DIM = 64
PEAKS = 256


EPSILON = 1e-06
HIGHEST = lax.Precision.HIGHEST


def extended(x, sides, width):
    for axis, dim in sides:
        peers, length = (lax.axis_size(axis), x.shape[dim])
        up = [(i, (i + 1) % peers) for i in range(peers - 1)]
        down = [(j, i) for i, j in up]
        last = lax.slice_in_dim(x, length - width, length, axis=dim)
        leading = lax.slice_in_dim(x, 0, width, axis=dim)
        before = lax.ppermute(last, axis, up)
        after = lax.ppermute(leading, axis, down)
        x = jnp.concatenate([before, x, after], axis=dim)
    return x


def swap_sec(x):
    return lax.ppermute(x, "sec", [(0, 1), (1, 0)])


def sum_sec(x):
    return x + swap_sec(x)


def sum_atoms(x):
    peers = lax.axis_size("atoms")
    flat = x.reshape(-1)
    chunk = -(-flat.shape[0] // (peers * 128)) * 128
    flat = jnp.pad(flat, (0, chunk * peers - flat.shape[0]))
    pieces = flat.reshape(peers, chunk // 128, 128)
    arrived = lax.all_to_all(pieces, "atoms", 0, 0, tiled=True)
    owned = jnp.sum(arrived, axis=0, keepdims=True)
    spread = lax.all_to_all(jnp.broadcast_to(owned, pieces.shape), "atoms", 0, 0, tiled=True)
    return spread.reshape(-1)[: x.size].reshape(x.shape)


def feature_map(values):
    return jax.nn.elu(values) + 1.0


def message_pass(atom_rows, tile_pair, tile_block):
    tile_size = tile_block.shape[-1]
    local_rows, half_width = atom_rows.shape
    block_count = local_rows // tile_size
    reach_blocks = max(block_count // 2, 1)
    padded = extended(atom_rows, (("atoms", 0),), reach_blocks * tile_size)
    blocks = padded.reshape(block_count + 2 * reach_blocks, tile_size, half_width)
    first_block = lax.axis_index("atoms") * block_count
    row_ids = tile_pair[0]
    col_ids = tile_pair[1]
    live_tiles = row_ids >= 0
    col_local = jnp.where(live_tiles, col_ids - first_block + reach_blocks, 0)
    row_local = jnp.where(live_tiles, row_ids - first_block, -1)
    panels = jnp.take(blocks, col_local, axis=0)
    selector = row_local[None, :] == jnp.arange(block_count, dtype=jnp.int32)[:, None]
    masked = jnp.where(selector[:, :, None, None], tile_block[None], jnp.zeros_like(tile_block[None]))
    summed = jnp.einsum("btij,tjf->bif", masked, panels, preferred_element_type=jnp.float32)
    return summed.reshape(local_rows, half_width).astype(jnp.bfloat16)


def key_summary(key_rows, value_rows, atom_mask, head_count):
    count_rows = key_rows.shape[0]
    feat_keys = (
        feature_map(key_rows.astype(jnp.float32)).reshape(count_rows, head_count, -1)
        * atom_mask[:, None, None]
    )
    value_f = value_rows.astype(jnp.float32).reshape(count_rows, head_count, -1)
    outer_state = jnp.einsum("nhd,nhe->hde", feat_keys, value_f, precision=HIGHEST)
    return (outer_state, jnp.sum(feat_keys, axis=0))


def read_summary(query_rows, outer_state, key_total, head_count):
    count_rows = query_rows.shape[0]
    feat_query = feature_map(query_rows.astype(jnp.float32)).reshape(count_rows, head_count, -1)
    numerator = jnp.einsum("nhd,hde->nhe", feat_query, outer_state, precision=HIGHEST)
    denominator = jnp.einsum("nhd,hd->nh", feat_query, key_total, precision=HIGHEST)
    return (numerator / denominator[..., None]).reshape(count_rows, -1)


def contrast(unit_rows, peak_rows, label_part, mask_part, peak_start):
    logit_scale = 2.0 / math.sqrt(unit_rows.shape[-1])
    peak_f = peak_rows.astype(jnp.float32)
    logits = logit_scale * jnp.dot(unit_rows, peak_f.T, precision=HIGHEST)
    peak_index = peak_start + jnp.arange(peak_rows.shape[0], dtype=jnp.int32)
    target = (label_part[:, None] == peak_index[None, :]).astype(jnp.float32)
    sign_rows = 2.0 * target - 1.0
    loss_part = jnp.sum(mask_part[:, None] * jax.nn.softplus(-sign_rows * logits)) / PEAKS
    slopes = mask_part[:, None] * (jax.nn.sigmoid(logits) - target) * (1.0 / math.sqrt(PEAKS))
    unit_grad = logit_scale * jnp.dot(slopes, peak_f, precision=HIGHEST)
    return (loss_part, unit_grad)


def embed_backward(unit_rows, unit_grad, embed_scale):
    inner_mean = jnp.mean(unit_grad * unit_rows, axis=-1, keepdims=True)
    return (embed_scale * (unit_grad - unit_rows * inner_mean)).astype(jnp.bfloat16)


def shards(
    atoms_in,
    tile_ids,
    tile_vals,
    seq_lens,
    pair_labels,
    peak_embed,
    norm_gain,
    w_query,
    w_key,
    w_value,
    w_out,
    w_proj,
):
    atom_rows = atoms_in[0]
    local_rows = atom_rows.shape[0]
    gathered = message_pass(atom_rows, tile_ids[0], tile_vals[0])
    hidden_one = (atom_rows.astype(jnp.float32) + gathered.astype(jnp.float32)).astype(jnp.bfloat16)
    atom_base = lax.axis_index("atoms") * local_rows
    length_one = seq_lens[0]
    label_row = pair_labels[0]
    peak_part = peak_embed[0]
    hidden_f = hidden_one.astype(jnp.float32)
    square_sum = lax.psum(jnp.sum(hidden_f * hidden_f, axis=-1), "sec")
    row_scale = lax.rsqrt(square_sum[:, None] / D + EPSILON)
    normed = (hidden_f * row_scale * norm_gain.astype(jnp.float32)).astype(jnp.bfloat16)
    head_cols = w_query.shape[1]
    sec = lax.axis_index("sec")
    width = normed.shape[1]
    other_rows = swap_sec(normed)

    def project(weight):
        halves = weight.reshape(2, width, weight.shape[1])
        mine = jnp.dot(normed, halves[sec], preferred_element_type=jnp.float32)
        return mine + jnp.dot(other_rows, halves[1 - sec], preferred_element_type=jnp.float32)

    query_f, key_f, value_f = tuple((project(weight) for weight in (w_query, w_key, w_value)))
    head_count = head_cols // HEAD_DIM
    atom_mask = (atom_base + jnp.arange(local_rows, dtype=jnp.int32) < length_one).astype(
        jnp.float32
    )
    outer_state, key_total = key_summary(
        key_f.astype(jnp.bfloat16), value_f.astype(jnp.bfloat16), atom_mask, head_count
    )
    state_rows = jnp.concatenate([outer_state, key_total[:, None, :]], axis=1)
    packed = sum_atoms(state_rows)
    outer_state, key_total = packed[:, :HEAD_DIM, :], packed[:, HEAD_DIM, :]
    attended = read_summary(query_f.astype(jnp.bfloat16), outer_state, key_total, head_count)
    out_sum = lax.psum(jnp.sum(attended * attended, axis=-1), "sec")
    attended_n = (attended * lax.rsqrt(out_sum[:, None] / (HEADS * HEAD_DIM) + EPSILON)).astype(
        jnp.bfloat16
    )
    out_cols = w_out.reshape(w_out.shape[0], 2, width)
    sent = jnp.dot(attended_n, out_cols[:, 1 - sec, :], preferred_element_type=jnp.float32)
    kept = jnp.dot(attended_n, out_cols[:, sec, :], preferred_element_type=jnp.float32)
    branch = kept + swap_sec(sent)
    hidden_two = (hidden_f + branch).astype(jnp.bfloat16)
    embedded = sum_sec(jnp.dot(hidden_two, w_proj, preferred_element_type=jnp.float32))
    embed_scale = lax.rsqrt(jnp.mean(embedded * embedded, axis=-1, keepdims=True) + EPSILON)
    unit_rows = embedded * embed_scale
    peak_start = sec * peak_part.shape[0]
    loss_part, unit_grad = contrast(unit_rows, peak_part, label_row, atom_mask, peak_start)
    unit_grad = sum_sec(unit_grad)
    embed_grad = embed_backward(unit_rows, unit_grad, embed_scale)
    proj_part = jnp.einsum("nd,ne->de", hidden_two, embed_grad, preferred_element_type=jnp.float32)
    loss_pair = sum_sec(loss_part)
    packed = sum_atoms(jnp.concatenate([proj_part.reshape(-1), loss_pair.reshape(1)]))
    proj_total = packed[: proj_part.size].reshape(proj_part.shape)
    loss_total = packed[proj_part.size] / (local_rows * lax.axis_size("atoms"))
    return (hidden_two[None], loss_total.reshape(1), proj_total[None])


def solution(mesh):
    return jax.shard_map(
        shards,
        mesh=mesh,
        in_specs=(
            P("batch", "atoms", "sec"),
            P("batch", None, "atoms"),
            P("batch", "atoms", None, None),
            P("batch"),
            P("batch", "atoms"),
            P("batch", "sec", None),
            P("sec"),
            P(None, "sec"),
            P(None, "sec"),
            P(None, "sec"),
            P("sec", None),
            P("sec", None),
        ),
        out_specs=(P("batch", "atoms", "sec"), P("batch"), P("batch", "sec", None)),
        check_vma=False,
    )
```

```python
import math

import jax
import jax.numpy as jnp
from jax import lax
from jax.sharding import PartitionSpec as P

D = 1024
HEADS = 8
HEAD_DIM = 64
PEAKS = 256


EPSILON = 1e-06
HIGHEST = lax.Precision.HIGHEST


def extended(x, sides, width):
    for axis, dim in sides:
        peers, length = (lax.axis_size(axis), x.shape[dim])
        up = [(i, (i + 1) % peers) for i in range(peers - 1)]
        down = [(j, i) for i, j in up]
        last = lax.slice_in_dim(x, length - width, length, axis=dim)
        leading = lax.slice_in_dim(x, 0, width, axis=dim)
        before = lax.ppermute(last, axis, up)
        after = lax.ppermute(leading, axis, down)
        x = jnp.concatenate([before, x, after], axis=dim)
    return x


def swap_sec(x):
    return lax.ppermute(x, "sec", [(0, 1), (1, 0)])


def join_sec(mine, other, sec, axis):
    first = jnp.where(sec == 0, mine, other)
    second = jnp.where(sec == 0, other, mine)
    return jnp.concatenate([first, second], axis=axis)


def sum_sec(x):
    return x + swap_sec(x)


def sum_atoms(x):
    peers = lax.axis_size("atoms")
    flat = x.reshape(-1)
    chunk = -(-flat.shape[0] // (peers * 128)) * 128
    flat = jnp.pad(flat, (0, chunk * peers - flat.shape[0]))
    pieces = flat.reshape(peers, chunk // 128, 128)
    arrived = lax.all_to_all(pieces, "atoms", 0, 0, tiled=True)
    owned = jnp.sum(arrived, axis=0, keepdims=True)
    spread = lax.all_to_all(jnp.broadcast_to(owned, pieces.shape), "atoms", 0, 0, tiled=True)
    return spread.reshape(-1)[: x.size].reshape(x.shape)


def feature_map(values):
    return jax.nn.elu(values) + 1.0


def message_pass(atom_rows, tile_pair, tile_block):
    tile_size = tile_block.shape[-1]
    local_rows, half_width = atom_rows.shape
    block_count = local_rows // tile_size
    reach_blocks = max(block_count // 2, 1)
    padded = extended(atom_rows, (("atoms", 0),), reach_blocks * tile_size)
    blocks = padded.reshape(block_count + 2 * reach_blocks, tile_size, half_width)
    first_block = lax.axis_index("atoms") * block_count
    row_ids = tile_pair[0]
    col_ids = tile_pair[1]
    live_tiles = row_ids >= 0
    col_local = jnp.where(live_tiles, col_ids - first_block + reach_blocks, 0)
    row_local = jnp.where(live_tiles, row_ids - first_block, -1)
    panels = jnp.take(blocks, col_local, axis=0)
    selector = row_local[None, :] == jnp.arange(block_count, dtype=jnp.int32)[:, None]
    masked = jnp.where(selector[:, :, None, None], tile_block[None], jnp.zeros_like(tile_block[None]))
    summed = jnp.einsum("btij,tjf->bif", masked, panels, preferred_element_type=jnp.float32)
    return summed.reshape(local_rows, half_width).astype(jnp.bfloat16)


def key_summary(key_rows, value_rows, atom_mask, head_count):
    count_rows = key_rows.shape[0]
    feat_keys = (
        feature_map(key_rows.astype(jnp.float32)).reshape(count_rows, head_count, -1)
        * atom_mask[:, None, None]
    )
    value_f = value_rows.astype(jnp.float32).reshape(count_rows, head_count, -1)
    outer_state = jnp.einsum("nhd,nhe->hde", feat_keys, value_f, precision=HIGHEST)
    return (outer_state, jnp.sum(feat_keys, axis=0))


def read_summary(query_rows, outer_state, key_total, head_count):
    count_rows = query_rows.shape[0]
    feat_query = feature_map(query_rows.astype(jnp.float32)).reshape(count_rows, head_count, -1)
    numerator = jnp.einsum("nhd,hde->nhe", feat_query, outer_state, precision=HIGHEST)
    denominator = jnp.einsum("nhd,hd->nh", feat_query, key_total, precision=HIGHEST)
    return (numerator / denominator[..., None]).reshape(count_rows, -1)


def contrast(unit_rows, peak_rows, label_part, mask_part, peak_start):
    logit_scale = 2.0 / math.sqrt(unit_rows.shape[-1])
    peak_f = peak_rows.astype(jnp.float32)
    logits = logit_scale * jnp.dot(unit_rows, peak_f.T, precision=HIGHEST)
    peak_index = peak_start + jnp.arange(peak_rows.shape[0], dtype=jnp.int32)
    target = (label_part[:, None] == peak_index[None, :]).astype(jnp.float32)
    sign_rows = 2.0 * target - 1.0
    loss_part = jnp.sum(mask_part[:, None] * jax.nn.softplus(-sign_rows * logits)) / PEAKS
    slopes = mask_part[:, None] * (jax.nn.sigmoid(logits) - target) * (1.0 / math.sqrt(PEAKS))
    unit_grad = logit_scale * jnp.dot(slopes, peak_f, precision=HIGHEST)
    return (loss_part, unit_grad)


def embed_backward(unit_rows, unit_grad, embed_scale):
    inner_mean = jnp.mean(unit_grad * unit_rows, axis=-1, keepdims=True)
    return (embed_scale * (unit_grad - unit_rows * inner_mean)).astype(jnp.bfloat16)


def shards(
    atoms_in,
    tile_ids,
    tile_vals,
    seq_lens,
    pair_labels,
    peak_embed,
    norm_gain,
    w_query,
    w_key,
    w_value,
    w_out,
    w_proj,
):
    atom_rows = atoms_in[0]
    local_rows = atom_rows.shape[0]
    gathered = message_pass(atom_rows, tile_ids[0], tile_vals[0])
    hidden_one = (atom_rows.astype(jnp.float32) + gathered.astype(jnp.float32)).astype(jnp.bfloat16)
    atom_base = lax.axis_index("atoms") * local_rows
    length_one = seq_lens[0]
    label_row = pair_labels[0]
    peak_part = peak_embed[0]
    hidden_f = hidden_one.astype(jnp.float32)
    square_sum = lax.psum(jnp.sum(hidden_f * hidden_f, axis=-1), "sec")
    row_scale = lax.rsqrt(square_sum[:, None] / D + EPSILON)
    normed = (hidden_f * row_scale * norm_gain.astype(jnp.float32)).astype(jnp.bfloat16)
    head_cols = w_query.shape[1]
    sec = lax.axis_index("sec")
    width = normed.shape[1]
    other_rows = swap_sec(normed)
    peak_all = join_sec(peak_part, swap_sec(peak_part), sec, 0)
    out_cols = w_out.reshape(w_out.shape[0], 2, width)
    out_rows = join_sec(out_cols[:, sec, :], swap_sec(out_cols[:, 1 - sec, :]), sec, 0)

    def project(weight):
        halves = weight.reshape(2, width, weight.shape[1])
        mine = jnp.dot(normed, halves[sec], preferred_element_type=jnp.float32)
        return mine + jnp.dot(other_rows, halves[1 - sec], preferred_element_type=jnp.float32)

    query_f, key_f, value_f = tuple((project(weight) for weight in (w_query, w_key, w_value)))
    head_count = head_cols // HEAD_DIM
    atom_mask = (atom_base + jnp.arange(local_rows, dtype=jnp.int32) < length_one).astype(
        jnp.float32
    )
    outer_state, key_total = key_summary(
        key_f.astype(jnp.bfloat16), value_f.astype(jnp.bfloat16), atom_mask, head_count
    )
    state_rows = jnp.concatenate([outer_state, key_total[:, None, :]], axis=1)
    packed = sum_atoms(state_rows)
    outer_state, key_total = packed[:, :HEAD_DIM, :], packed[:, HEAD_DIM, :]
    attended = read_summary(query_f.astype(jnp.bfloat16), outer_state, key_total, head_count)
    attended_all = join_sec(attended, swap_sec(attended), sec, 1)
    out_sum = jnp.sum(attended_all * attended_all, axis=-1)
    attended_n = (attended_all * lax.rsqrt(out_sum[:, None] / (HEADS * HEAD_DIM) + EPSILON)).astype(
        jnp.bfloat16
    )
    branch = jnp.dot(attended_n, out_rows, preferred_element_type=jnp.float32)
    hidden_two = (hidden_f + branch).astype(jnp.bfloat16)
    embedded = sum_sec(jnp.dot(hidden_two, w_proj, preferred_element_type=jnp.float32))
    embed_scale = lax.rsqrt(jnp.mean(embedded * embedded, axis=-1, keepdims=True) + EPSILON)
    unit_rows = embedded * embed_scale
    loss_part, unit_grad = contrast(unit_rows, peak_all, label_row, atom_mask, 0)
    embed_grad = embed_backward(unit_rows, unit_grad, embed_scale)
    proj_part = jnp.einsum("nd,ne->de", hidden_two, embed_grad, preferred_element_type=jnp.float32)
    packed = sum_atoms(jnp.concatenate([proj_part.reshape(-1), loss_part.reshape(1)]))
    proj_total = packed[: proj_part.size].reshape(proj_part.shape)
    loss_total = packed[proj_part.size] / (local_rows * lax.axis_size("atoms"))
    return (hidden_two[None], loss_total.reshape(1), proj_total[None])


def solution(mesh):
    return jax.shard_map(
        shards,
        mesh=mesh,
        in_specs=(
            P("batch", "atoms", "sec"),
            P("batch", None, "atoms"),
            P("batch", "atoms", None, None),
            P("batch"),
            P("batch", "atoms"),
            P("batch", "sec", None),
            P("sec"),
            P(None, "sec"),
            P(None, "sec"),
            P(None, "sec"),
            P("sec", None),
            P("sec", None),
        ),
        out_specs=(P("batch", "atoms", "sec"), P("batch"), P("batch", "sec", None)),
        check_vma=False,
    )
```

```python
import math

import jax
import jax.numpy as jnp
from jax import lax
from jax.sharding import PartitionSpec as P

D = 1024
HEADS = 8
HEAD_DIM = 64
PEAKS = 256


EPSILON = 1e-06
HIGHEST = lax.Precision.HIGHEST


def extended(x, sides, width):
    for axis, dim in sides:
        peers, length = (lax.axis_size(axis), x.shape[dim])
        up = [(i, (i + 1) % peers) for i in range(peers - 1)]
        down = [(j, i) for i, j in up]
        last = lax.slice_in_dim(x, length - width, length, axis=dim)
        leading = lax.slice_in_dim(x, 0, width, axis=dim)
        before = lax.ppermute(last, axis, up)
        after = lax.ppermute(leading, axis, down)
        x = jnp.concatenate([before, x, after], axis=dim)
    return x


def swap_sec(x):
    return lax.ppermute(x, "sec", [(0, 1), (1, 0)])


def join_sec(mine, other, sec, axis):
    first = jnp.where(sec == 0, mine, other)
    second = jnp.where(sec == 0, other, mine)
    return jnp.concatenate([first, second], axis=axis)


def sum_atoms(x):
    peers = lax.axis_size("atoms")
    flat = x.reshape(-1)
    chunk = -(-flat.shape[0] // (peers * 128)) * 128
    flat = jnp.pad(flat, (0, chunk * peers - flat.shape[0]))
    pieces = flat.reshape(peers, chunk // 128, 128)
    arrived = lax.all_to_all(pieces, "atoms", 0, 0, tiled=True)
    owned = jnp.sum(arrived, axis=0, keepdims=True)
    spread = lax.all_to_all(jnp.broadcast_to(owned, pieces.shape), "atoms", 0, 0, tiled=True)
    return spread.reshape(-1)[: x.size].reshape(x.shape)


def feature_map(values):
    return jax.nn.elu(values) + 1.0


def message_pass(atom_rows, tile_pair, tile_block):
    tile_size = tile_block.shape[-1]
    local_rows, half_width = atom_rows.shape
    block_count = local_rows // tile_size
    reach_blocks = max(block_count // 2, 1)
    padded = extended(atom_rows, (("atoms", 0),), reach_blocks * tile_size)
    blocks = padded.reshape(block_count + 2 * reach_blocks, tile_size, half_width)
    first_block = lax.axis_index("atoms") * block_count
    row_ids = tile_pair[0]
    col_ids = tile_pair[1]
    live_tiles = row_ids >= 0
    col_local = jnp.where(live_tiles, col_ids - first_block + reach_blocks, 0)
    row_local = jnp.where(live_tiles, row_ids - first_block, -1)
    panels = jnp.take(blocks, col_local, axis=0)
    selector = row_local[None, :] == jnp.arange(block_count, dtype=jnp.int32)[:, None]
    masked = jnp.where(selector[:, :, None, None], tile_block[None], jnp.zeros_like(tile_block[None]))
    summed = jnp.einsum("btij,tjf->bif", masked, panels, preferred_element_type=jnp.float32)
    return summed.reshape(local_rows, half_width).astype(jnp.bfloat16)


def key_summary(key_rows, value_rows, atom_mask, head_count):
    count_rows = key_rows.shape[0]
    feat_keys = (
        feature_map(key_rows.astype(jnp.float32)).reshape(count_rows, head_count, -1)
        * atom_mask[:, None, None]
    )
    value_f = value_rows.astype(jnp.float32).reshape(count_rows, head_count, -1)
    outer_state = jnp.einsum("nhd,nhe->hde", feat_keys, value_f, precision=HIGHEST)
    return (outer_state, jnp.sum(feat_keys, axis=0))


def read_summary(query_rows, outer_state, key_total, head_count):
    count_rows = query_rows.shape[0]
    feat_query = feature_map(query_rows.astype(jnp.float32)).reshape(count_rows, head_count, -1)
    numerator = jnp.einsum("nhd,hde->nhe", feat_query, outer_state, precision=HIGHEST)
    denominator = jnp.einsum("nhd,hd->nh", feat_query, key_total, precision=HIGHEST)
    return (numerator / denominator[..., None]).reshape(count_rows, -1)


def contrast(unit_rows, peak_rows, label_part, mask_part, peak_start):
    logit_scale = 2.0 / math.sqrt(unit_rows.shape[-1])
    peak_f = peak_rows.astype(jnp.float32)
    logits = logit_scale * jnp.dot(unit_rows, peak_f.T, precision=HIGHEST)
    peak_index = peak_start + jnp.arange(peak_rows.shape[0], dtype=jnp.int32)
    target = (label_part[:, None] == peak_index[None, :]).astype(jnp.float32)
    sign_rows = 2.0 * target - 1.0
    loss_part = jnp.sum(mask_part[:, None] * jax.nn.softplus(-sign_rows * logits)) / PEAKS
    slopes = mask_part[:, None] * (jax.nn.sigmoid(logits) - target) * (1.0 / math.sqrt(PEAKS))
    unit_grad = logit_scale * jnp.dot(slopes, peak_f, precision=HIGHEST)
    return (loss_part, unit_grad)


def embed_backward(unit_rows, unit_grad, embed_scale):
    inner_mean = jnp.mean(unit_grad * unit_rows, axis=-1, keepdims=True)
    return (embed_scale * (unit_grad - unit_rows * inner_mean)).astype(jnp.bfloat16)


def shards(
    atoms_in,
    tile_ids,
    tile_vals,
    seq_lens,
    pair_labels,
    peak_embed,
    norm_gain,
    w_query,
    w_key,
    w_value,
    w_out,
    w_proj,
):
    atom_rows = atoms_in[0]
    local_rows, width = atom_rows.shape
    sec = lax.axis_index("sec")
    peak_part = peak_embed[0]
    partner = swap_sec((norm_gain, peak_part, w_out, w_proj))
    gain_all, peak_all, out_all, proj_all = (
        join_sec(mine, other, sec, 0)
        for mine, other in zip((norm_gain, peak_part, w_out, w_proj), partner)
    )
    gathered = message_pass(atom_rows, tile_ids[0], tile_vals[0])
    hidden_one = (atom_rows.astype(jnp.float32) + gathered.astype(jnp.float32)).astype(jnp.bfloat16)
    hidden_f = join_sec(hidden_one, swap_sec(hidden_one), sec, 1).astype(jnp.float32)
    atom_base = lax.axis_index("atoms") * local_rows
    length_one = seq_lens[0]
    label_row = pair_labels[0]
    row_scale = lax.rsqrt(jnp.mean(hidden_f * hidden_f, axis=-1, keepdims=True) + EPSILON)
    normed = (hidden_f * row_scale * gain_all.astype(jnp.float32)).astype(jnp.bfloat16)
    head_cols = w_query.shape[1]
    query_f, key_f, value_f = tuple(
        (
            jnp.dot(normed, weight, preferred_element_type=jnp.float32)
            for weight in (w_query, w_key, w_value)
        )
    )
    head_count = head_cols // HEAD_DIM
    atom_mask = (atom_base + jnp.arange(local_rows, dtype=jnp.int32) < length_one).astype(
        jnp.float32
    )
    outer_state, key_total = key_summary(
        key_f.astype(jnp.bfloat16), value_f.astype(jnp.bfloat16), atom_mask, head_count
    )
    state_rows = jnp.concatenate([outer_state, key_total[:, None, :]], axis=1)
    packed = sum_atoms(state_rows)
    outer_state, key_total = packed[:, :HEAD_DIM, :], packed[:, HEAD_DIM, :]
    attended = read_summary(query_f.astype(jnp.bfloat16), outer_state, key_total, head_count)
    attended_all = join_sec(attended, swap_sec(attended), sec, 1)
    out_scale = lax.rsqrt(jnp.mean(attended_all * attended_all, axis=-1, keepdims=True) + EPSILON)
    attended_n = (attended_all * out_scale).astype(jnp.bfloat16)
    branch = jnp.dot(attended_n, out_all, preferred_element_type=jnp.float32)
    hidden_all = (hidden_f + branch).astype(jnp.bfloat16)
    embedded = jnp.dot(hidden_all, proj_all, preferred_element_type=jnp.float32)
    embed_scale = lax.rsqrt(jnp.mean(embedded * embedded, axis=-1, keepdims=True) + EPSILON)
    unit_rows = embedded * embed_scale
    loss_part, unit_grad = contrast(unit_rows, peak_all, label_row, atom_mask, 0)
    embed_grad = embed_backward(unit_rows, unit_grad, embed_scale)
    hidden_two = lax.dynamic_slice_in_dim(hidden_all, sec * width, width, axis=1)
    proj_part = jnp.einsum("nd,ne->de", hidden_two, embed_grad, preferred_element_type=jnp.float32)
    packed = sum_atoms(jnp.concatenate([proj_part.reshape(-1), loss_part.reshape(1)]))
    proj_total = packed[: proj_part.size].reshape(proj_part.shape)
    loss_total = packed[proj_part.size] / (local_rows * lax.axis_size("atoms"))
    return (hidden_two[None], loss_total.reshape(1), proj_total[None])


def solution(mesh):
    return jax.shard_map(
        shards,
        mesh=mesh,
        in_specs=(
            P("batch", "atoms", "sec"),
            P("batch", None, "atoms"),
            P("batch", "atoms", None, None),
            P("batch"),
            P("batch", "atoms"),
            P("batch", "sec", None),
            P("sec"),
            P(None, "sec"),
            P(None, "sec"),
            P(None, "sec"),
            P("sec", None),
            P("sec", None),
        ),
        out_specs=(P("batch", "atoms", "sec"), P("batch"), P("batch", "sec", None)),
        check_vma=False,
    )
```

```python
import math

import jax
import jax.numpy as jnp
from jax import lax
from jax.sharding import PartitionSpec as P

D = 1024
HEADS = 8
HEAD_DIM = 64
PEAKS = 256


EPSILON = 1e-06
HIGHEST = lax.Precision.HIGHEST


def extended(x, sides, width):
    for axis, dim in sides:
        peers, length = (lax.axis_size(axis), x.shape[dim])
        up = [(i, (i + 1) % peers) for i in range(peers - 1)]
        down = [(j, i) for i, j in up]
        last = lax.slice_in_dim(x, length - width, length, axis=dim)
        leading = lax.slice_in_dim(x, 0, width, axis=dim)
        before = lax.ppermute(last, axis, up)
        after = lax.ppermute(leading, axis, down)
        x = jnp.concatenate([before, x, after], axis=dim)
    return x


def swap_sec(x):
    return lax.ppermute(x, "sec", [(0, 1), (1, 0)])


def sum_atoms(x):
    peers = lax.axis_size("atoms")
    flat = x.reshape(-1)
    chunk = -(-flat.shape[0] // (peers * 128)) * 128
    flat = jnp.pad(flat, (0, chunk * peers - flat.shape[0]))
    pieces = flat.reshape(peers, chunk // 128, 128)
    arrived = lax.all_to_all(pieces, "atoms", 0, 0, tiled=True)
    owned = jnp.sum(arrived, axis=0, keepdims=True)
    spread = lax.all_to_all(jnp.broadcast_to(owned, pieces.shape), "atoms", 0, 0, tiled=True)
    return spread.reshape(-1)[: x.size].reshape(x.shape)


def feature_map(values):
    return jax.nn.elu(values) + 1.0


def message_pass(atom_rows, tile_pair, tile_block):
    tile_size = tile_block.shape[-1]
    local_rows, half_width = atom_rows.shape
    block_count = local_rows // tile_size
    reach_blocks = max(block_count // 2, 1)
    padded = extended(atom_rows, (("atoms", 0),), reach_blocks * tile_size)
    blocks = padded.reshape(block_count + 2 * reach_blocks, tile_size, half_width)
    first_block = lax.axis_index("atoms") * block_count
    row_ids = tile_pair[0]
    col_ids = tile_pair[1]
    live_tiles = row_ids >= 0
    col_local = jnp.where(live_tiles, col_ids - first_block + reach_blocks, 0)
    row_local = jnp.where(live_tiles, row_ids - first_block, -1)
    panels = jnp.take(blocks, col_local, axis=0)
    selector = row_local[None, :] == jnp.arange(block_count, dtype=jnp.int32)[:, None]
    masked = jnp.where(selector[:, :, None, None], tile_block[None], jnp.zeros_like(tile_block[None]))
    summed = jnp.einsum("btij,tjf->bif", masked, panels, preferred_element_type=jnp.float32)
    return summed.reshape(local_rows, half_width).astype(jnp.bfloat16)


def key_summary(key_rows, value_rows, atom_mask, head_count):
    count_rows = key_rows.shape[0]
    feat_keys = (
        feature_map(key_rows.astype(jnp.float32)).reshape(count_rows, head_count, -1)
        * atom_mask[:, None, None]
    )
    value_f = value_rows.astype(jnp.float32).reshape(count_rows, head_count, -1)
    outer_state = jnp.einsum("nhd,nhe->hde", feat_keys, value_f, precision=HIGHEST)
    return (outer_state, jnp.sum(feat_keys, axis=0))


def read_summary(query_rows, outer_state, key_total, head_count):
    count_rows = query_rows.shape[0]
    feat_query = feature_map(query_rows.astype(jnp.float32)).reshape(count_rows, head_count, -1)
    numerator = jnp.einsum("nhd,hde->nhe", feat_query, outer_state, precision=HIGHEST)
    denominator = jnp.einsum("nhd,hd->nh", feat_query, key_total, precision=HIGHEST)
    return (numerator / denominator[..., None]).reshape(count_rows, -1)


def contrast(unit_rows, peak_rows, label_part, mask_part, peak_start):
    logit_scale = 2.0 / math.sqrt(unit_rows.shape[-1])
    peak_f = peak_rows.astype(jnp.float32)
    logits = logit_scale * jnp.dot(unit_rows, peak_f.T, precision=HIGHEST)
    peak_index = peak_start + jnp.arange(peak_rows.shape[0], dtype=jnp.int32)
    target = (label_part[:, None] == peak_index[None, :]).astype(jnp.float32)
    sign_rows = 2.0 * target - 1.0
    loss_part = jnp.sum(mask_part[:, None] * jax.nn.softplus(-sign_rows * logits)) / PEAKS
    slopes = mask_part[:, None] * (jax.nn.sigmoid(logits) - target) * (1.0 / math.sqrt(PEAKS))
    unit_grad = logit_scale * jnp.dot(slopes, peak_f, precision=HIGHEST)
    return (loss_part, unit_grad)


def embed_backward(unit_rows, unit_grad, embed_scale):
    inner_mean = jnp.mean(unit_grad * unit_rows, axis=-1, keepdims=True)
    return (embed_scale * (unit_grad - unit_rows * inner_mean)).astype(jnp.bfloat16)


def shards(
    atoms_in,
    tile_ids,
    tile_vals,
    seq_lens,
    pair_labels,
    peak_embed,
    norm_gain,
    w_query,
    w_key,
    w_value,
    w_out,
    w_proj,
):
    atom_rows = atoms_in[0]
    local_rows, width = atom_rows.shape
    sec = lax.axis_index("sec")
    peak_part = peak_embed[0]
    statics = (norm_gain, peak_part, w_out, w_proj)
    arrived = swap_sec(jnp.concatenate([piece.reshape(-1) for piece in statics]))
    offsets = [0]
    for piece in statics:
        offsets.append(offsets[-1] + piece.size)
    gain_other, peak_other, out_other, proj_other = (
        arrived[start:stop].reshape(piece.shape)
        for piece, start, stop in zip(statics, offsets[:-1], offsets[1:])
    )
    gathered = message_pass(atom_rows, tile_ids[0], tile_vals[0])
    hidden_one = (atom_rows.astype(jnp.float32) + gathered.astype(jnp.float32)).astype(jnp.bfloat16)
    mine_f = hidden_one.astype(jnp.float32)
    other_f = swap_sec(hidden_one).astype(jnp.float32)
    atom_base = lax.axis_index("atoms") * local_rows
    length_one = seq_lens[0]
    label_row = pair_labels[0]
    square_sum = jnp.sum(mine_f * mine_f, axis=-1, keepdims=True) + jnp.sum(
        other_f * other_f, axis=-1, keepdims=True
    )
    row_scale = lax.rsqrt(square_sum / D + EPSILON)
    normed_mine = (mine_f * row_scale * norm_gain.astype(jnp.float32)).astype(jnp.bfloat16)
    normed_other = (other_f * row_scale * gain_other.astype(jnp.float32)).astype(jnp.bfloat16)
    head_cols = w_query.shape[1]

    def project(weight):
        halves = weight.reshape(2, width, weight.shape[1])
        mine = jnp.dot(normed_mine, halves[sec], preferred_element_type=jnp.float32)
        return mine + jnp.dot(normed_other, halves[1 - sec], preferred_element_type=jnp.float32)

    query_f, key_f, value_f = tuple((project(weight) for weight in (w_query, w_key, w_value)))
    head_count = head_cols // HEAD_DIM
    atom_mask = (atom_base + jnp.arange(local_rows, dtype=jnp.int32) < length_one).astype(
        jnp.float32
    )
    outer_state, key_total = key_summary(
        key_f.astype(jnp.bfloat16), value_f.astype(jnp.bfloat16), atom_mask, head_count
    )
    state_rows = jnp.concatenate([outer_state, key_total[:, None, :]], axis=1)
    packed = sum_atoms(state_rows)
    outer_state, key_total = packed[:, :HEAD_DIM, :], packed[:, HEAD_DIM, :]
    attended = read_summary(query_f.astype(jnp.bfloat16), outer_state, key_total, head_count)
    attended_other = swap_sec(attended)
    out_sum = jnp.sum(attended * attended, axis=-1, keepdims=True) + jnp.sum(
        attended_other * attended_other, axis=-1, keepdims=True
    )
    out_scale = lax.rsqrt(out_sum / (HEADS * HEAD_DIM) + EPSILON)
    branch = jnp.dot(
        (attended * out_scale).astype(jnp.bfloat16), w_out, preferred_element_type=jnp.float32
    ) + jnp.dot(
        (attended_other * out_scale).astype(jnp.bfloat16), out_other, preferred_element_type=jnp.float32
    )
    branch_cols = branch.reshape(local_rows, 2, width)
    hidden_two = (mine_f + branch_cols[:, sec, :]).astype(jnp.bfloat16)
    hidden_other = (other_f + branch_cols[:, 1 - sec, :]).astype(jnp.bfloat16)
    embedded = jnp.dot(hidden_two, w_proj, preferred_element_type=jnp.float32) + jnp.dot(
        hidden_other, proj_other, preferred_element_type=jnp.float32
    )
    embed_scale = lax.rsqrt(jnp.mean(embedded * embedded, axis=-1, keepdims=True) + EPSILON)
    unit_rows = embedded * embed_scale
    peak_count = peak_part.shape[0]
    loss_mine, grad_mine = contrast(unit_rows, peak_part, label_row, atom_mask, sec * peak_count)
    loss_other, grad_other = contrast(
        unit_rows, peak_other, label_row, atom_mask, (1 - sec) * peak_count
    )
    loss_part = loss_mine + loss_other
    embed_grad = embed_backward(unit_rows, grad_mine + grad_other, embed_scale)
    proj_part = jnp.einsum("nd,ne->de", hidden_two, embed_grad, preferred_element_type=jnp.float32)
    packed = sum_atoms(jnp.concatenate([proj_part.reshape(-1), loss_part.reshape(1)]))
    proj_total = packed[: proj_part.size].reshape(proj_part.shape)
    loss_total = packed[proj_part.size] / (local_rows * lax.axis_size("atoms"))
    return (hidden_two[None], loss_total.reshape(1), proj_total[None])


def solution(mesh):
    return jax.shard_map(
        shards,
        mesh=mesh,
        in_specs=(
            P("batch", "atoms", "sec"),
            P("batch", None, "atoms"),
            P("batch", "atoms", None, None),
            P("batch"),
            P("batch", "atoms"),
            P("batch", "sec", None),
            P("sec"),
            P(None, "sec"),
            P(None, "sec"),
            P(None, "sec"),
            P("sec", None),
            P("sec", None),
        ),
        out_specs=(P("batch", "atoms", "sec"), P("batch"), P("batch", "sec", None)),
        check_vma=False,
    )
```

```python
import math

import jax
import jax.numpy as jnp
from jax import lax
from jax.sharding import PartitionSpec as P

D = 1024
HEADS = 8
HEAD_DIM = 64
PEAKS = 256


EPSILON = 1e-06
HIGHEST = lax.Precision.HIGHEST


def extended(x, sides, width):
    for axis, dim in sides:
        peers, length = (lax.axis_size(axis), x.shape[dim])
        up = [(i, (i + 1) % peers) for i in range(peers - 1)]
        down = [(j, i) for i, j in up]
        last = lax.slice_in_dim(x, length - width, length, axis=dim)
        leading = lax.slice_in_dim(x, 0, width, axis=dim)
        before = lax.ppermute(last, axis, up)
        after = lax.ppermute(leading, axis, down)
        x = jnp.concatenate([before, x, after], axis=dim)
    return x


def swap_sec(x):
    return lax.ppermute(x, "sec", [(0, 1), (1, 0)])


def join_sec(mine, other, sec, axis):
    first = jnp.where(sec == 0, mine, other)
    second = jnp.where(sec == 0, other, mine)
    return jnp.concatenate([first, second], axis=axis)


def sum_sec(x):
    return x + swap_sec(x)


def sum_atoms(x, exact=None):
    peers = lax.axis_size("atoms")
    flat = x.reshape(-1)
    chunk = -(-flat.shape[0] // (peers * 128)) * 128
    flat = jnp.pad(flat, (0, chunk * peers - flat.shape[0]))
    pieces = flat.reshape(peers, chunk // 128, 128)
    arrived = lax.all_to_all(pieces, "atoms", 0, 0, tiled=True)
    owned = jnp.sum(arrived, axis=0, keepdims=True)
    if exact is not None:
        owner, slot = divmod(exact, chunk)
        rest = owned - owned.astype(jnp.bfloat16).astype(jnp.float32)
        here = lax.axis_index("atoms") == owner
        spare = (slot + 1) // 128, (slot + 1) % 128
        kept = jnp.where(here, rest[0, slot // 128, slot % 128], owned[0, spare[0], spare[1]])
        owned = owned.at[0, spare[0], spare[1]].set(kept).astype(jnp.bfloat16)
    spread = lax.all_to_all(jnp.broadcast_to(owned, pieces.shape), "atoms", 0, 0, tiled=True)
    return spread.reshape(-1)[: x.size].reshape(x.shape).astype(jnp.float32)


def feature_map(values):
    return jax.nn.elu(values) + 1.0


def message_pass(atom_rows, tile_pair, tile_block):
    tile_size = tile_block.shape[-1]
    local_rows, half_width = atom_rows.shape
    block_count = local_rows // tile_size
    reach_blocks = max(block_count // 2, 1)
    padded = extended(atom_rows, (("atoms", 0),), reach_blocks * tile_size)
    blocks = padded.reshape(block_count + 2 * reach_blocks, tile_size, half_width)
    first_block = lax.axis_index("atoms") * block_count
    row_ids = tile_pair[0]
    col_ids = tile_pair[1]
    live_tiles = row_ids >= 0
    col_local = jnp.where(live_tiles, col_ids - first_block + reach_blocks, 0)
    row_local = jnp.where(live_tiles, row_ids - first_block, -1)
    panels = jnp.take(blocks, col_local, axis=0)
    selector = row_local[None, :] == jnp.arange(block_count, dtype=jnp.int32)[:, None]
    masked = jnp.where(selector[:, :, None, None], tile_block[None], jnp.zeros_like(tile_block[None]))
    summed = jnp.einsum("btij,tjf->bif", masked, panels, preferred_element_type=jnp.float32)
    return summed.reshape(local_rows, half_width).astype(jnp.bfloat16)


def key_summary(key_rows, value_rows, atom_mask, head_count):
    count_rows = key_rows.shape[0]
    feat_keys = (
        feature_map(key_rows.astype(jnp.float32)).reshape(count_rows, head_count, -1)
        * atom_mask[:, None, None]
    )
    value_f = value_rows.astype(jnp.float32).reshape(count_rows, head_count, -1)
    outer_state = jnp.einsum("nhd,nhe->hde", feat_keys, value_f, precision=HIGHEST)
    return (outer_state, jnp.sum(feat_keys, axis=0))


def read_summary(query_rows, outer_state, key_total, head_count):
    count_rows = query_rows.shape[0]
    feat_query = feature_map(query_rows.astype(jnp.float32)).reshape(count_rows, head_count, -1)
    numerator = jnp.einsum("nhd,hde->nhe", feat_query, outer_state, precision=HIGHEST)
    denominator = jnp.einsum("nhd,hd->nh", feat_query, key_total, precision=HIGHEST)
    return (numerator / denominator[..., None]).reshape(count_rows, -1)


def contrast(unit_rows, peak_rows, label_part, mask_part, peak_start):
    logit_scale = 2.0 / math.sqrt(unit_rows.shape[-1])
    peak_f = peak_rows.astype(jnp.float32)
    logits = logit_scale * jnp.dot(unit_rows, peak_f.T, precision=HIGHEST)
    peak_index = peak_start + jnp.arange(peak_rows.shape[0], dtype=jnp.int32)
    target = (label_part[:, None] == peak_index[None, :]).astype(jnp.float32)
    sign_rows = 2.0 * target - 1.0
    loss_part = jnp.sum(mask_part[:, None] * jax.nn.softplus(-sign_rows * logits)) / PEAKS
    slopes = mask_part[:, None] * (jax.nn.sigmoid(logits) - target) * (1.0 / math.sqrt(PEAKS))
    unit_grad = logit_scale * jnp.dot(slopes, peak_f, precision=HIGHEST)
    return (loss_part, unit_grad)


def embed_backward(unit_rows, unit_grad, embed_scale):
    inner_mean = jnp.mean(unit_grad * unit_rows, axis=-1, keepdims=True)
    return (embed_scale * (unit_grad - unit_rows * inner_mean)).astype(jnp.bfloat16)


def shards(
    atoms_in,
    tile_ids,
    tile_vals,
    seq_lens,
    pair_labels,
    peak_embed,
    norm_gain,
    w_query,
    w_key,
    w_value,
    w_out,
    w_proj,
):
    atom_rows = atoms_in[0]
    local_rows = atom_rows.shape[0]
    gathered = message_pass(atom_rows, tile_ids[0], tile_vals[0])
    hidden_one = (atom_rows.astype(jnp.float32) + gathered.astype(jnp.float32)).astype(jnp.bfloat16)
    atom_base = lax.axis_index("atoms") * local_rows
    length_one = seq_lens[0]
    label_row = pair_labels[0]
    peak_part = peak_embed[0]
    hidden_f = hidden_one.astype(jnp.float32)
    square_sum = lax.psum(jnp.sum(hidden_f * hidden_f, axis=-1), "sec")
    row_scale = lax.rsqrt(square_sum[:, None] / D + EPSILON)
    normed = (hidden_f * row_scale * norm_gain.astype(jnp.float32)).astype(jnp.bfloat16)
    head_cols = w_query.shape[1]
    sec = lax.axis_index("sec")
    width = normed.shape[1]
    other_rows = swap_sec(normed)
    peak_all = join_sec(peak_part, swap_sec(peak_part), sec, 0)
    out_cols = w_out.reshape(w_out.shape[0], 2, width)
    out_rows = join_sec(out_cols[:, sec, :], swap_sec(out_cols[:, 1 - sec, :]), sec, 0)

    def project(weight):
        halves = weight.reshape(2, width, weight.shape[1])
        mine = jnp.dot(normed, halves[sec], preferred_element_type=jnp.float32)
        return mine + jnp.dot(other_rows, halves[1 - sec], preferred_element_type=jnp.float32)

    query_f, key_f, value_f = tuple((project(weight) for weight in (w_query, w_key, w_value)))
    head_count = head_cols // HEAD_DIM
    atom_mask = (atom_base + jnp.arange(local_rows, dtype=jnp.int32) < length_one).astype(
        jnp.float32
    )
    outer_state, key_total = key_summary(
        key_f.astype(jnp.bfloat16), value_f.astype(jnp.bfloat16), atom_mask, head_count
    )
    state_rows = jnp.concatenate([outer_state, key_total[:, None, :]], axis=1)
    packed = sum_atoms(state_rows)
    outer_state, key_total = packed[:, :HEAD_DIM, :], packed[:, HEAD_DIM, :]
    attended = read_summary(query_f.astype(jnp.bfloat16), outer_state, key_total, head_count)
    attended_all = join_sec(attended, swap_sec(attended), sec, 1)
    out_sum = jnp.sum(attended_all * attended_all, axis=-1)
    attended_n = (attended_all * lax.rsqrt(out_sum[:, None] / (HEADS * HEAD_DIM) + EPSILON)).astype(
        jnp.bfloat16
    )
    branch = jnp.dot(attended_n, out_rows, preferred_element_type=jnp.float32)
    hidden_two = (hidden_f + branch).astype(jnp.bfloat16)
    embedded = sum_sec(jnp.dot(hidden_two, w_proj, preferred_element_type=jnp.float32))
    embed_scale = lax.rsqrt(jnp.mean(embedded * embedded, axis=-1, keepdims=True) + EPSILON)
    unit_rows = embedded * embed_scale
    loss_part, unit_grad = contrast(unit_rows, peak_all, label_row, atom_mask, 0)
    embed_grad = embed_backward(unit_rows, unit_grad, embed_scale)
    proj_part = jnp.einsum("nd,ne->de", hidden_two, embed_grad, preferred_element_type=jnp.float32)
    zero = jnp.zeros((1,), jnp.float32)
    payload = jnp.concatenate([proj_part.reshape(-1), loss_part.reshape(1), zero])
    packed = sum_atoms(payload, exact=proj_part.size)
    proj_total = packed[: proj_part.size].reshape(proj_part.shape)
    loss_sum = packed[proj_part.size] + packed[proj_part.size + 1]
    loss_total = loss_sum / (local_rows * lax.axis_size("atoms"))
    return (hidden_two[None], loss_total.reshape(1), proj_total[None])


def solution(mesh):
    return jax.shard_map(
        shards,
        mesh=mesh,
        in_specs=(
            P("batch", "atoms", "sec"),
            P("batch", None, "atoms"),
            P("batch", "atoms", None, None),
            P("batch"),
            P("batch", "atoms"),
            P("batch", "sec", None),
            P("sec"),
            P(None, "sec"),
            P(None, "sec"),
            P(None, "sec"),
            P("sec", None),
            P("sec", None),
        ),
        out_specs=(P("batch", "atoms", "sec"), P("batch"), P("batch", "sec", None)),
        check_vma=False,
    )
```

```python
import math

import jax
import jax.numpy as jnp
from jax import lax
from jax.sharding import PartitionSpec as P

D = 1024
HEADS = 8
HEAD_DIM = 64
PEAKS = 256


EPSILON = 1e-06
HIGHEST = lax.Precision.HIGHEST


def extended(x, sides, width):
    for axis, dim in sides:
        peers, length = (lax.axis_size(axis), x.shape[dim])
        up = [(i, (i + 1) % peers) for i in range(peers - 1)]
        down = [(j, i) for i, j in up]
        last = lax.slice_in_dim(x, length - width, length, axis=dim)
        leading = lax.slice_in_dim(x, 0, width, axis=dim)
        before = lax.ppermute(last, axis, up)
        after = lax.ppermute(leading, axis, down)
        x = jnp.concatenate([before, x, after], axis=dim)
    return x


def swap_sec(x):
    return lax.ppermute(x, "sec", [(0, 1), (1, 0)])


def join_sec(mine, other, sec, axis):
    first = jnp.where(sec == 0, mine, other)
    second = jnp.where(sec == 0, other, mine)
    return jnp.concatenate([first, second], axis=axis)


def sum_sec(x):
    return x + swap_sec(x)


def sum_atoms(x, exact=None, riders=None):
    peers = lax.axis_size("atoms")
    flat = x.reshape(-1)
    chunk = -(-flat.shape[0] // (peers * 128)) * 128
    flat = jnp.pad(flat, (0, chunk * peers - flat.shape[0]))
    pieces = flat.reshape(peers, chunk // 128, 128)
    arrived = lax.all_to_all(pieces, "atoms", 0, 0, tiled=True)
    if riders is not None:
        arrived, riders = lax.optimization_barrier((arrived, riders))
    owned = jnp.sum(arrived, axis=0, keepdims=True)
    if exact is not None:
        owner, slot = divmod(exact, chunk)
        rest = owned - owned.astype(jnp.bfloat16).astype(jnp.float32)
        here = lax.axis_index("atoms") == owner
        spare = (slot + 1) // 128, (slot + 1) % 128
        kept = jnp.where(here, rest[0, slot // 128, slot % 128], owned[0, spare[0], spare[1]])
        owned = owned.at[0, spare[0], spare[1]].set(kept).astype(jnp.bfloat16)
    spread = lax.all_to_all(jnp.broadcast_to(owned, pieces.shape), "atoms", 0, 0, tiled=True)
    total = spread.reshape(-1)[: x.size].reshape(x.shape).astype(jnp.float32)
    return total if riders is None else (total, riders)


def feature_map(values):
    return jax.nn.elu(values) + 1.0


def message_pass(atom_rows, tile_pair, tile_block):
    tile_size = tile_block.shape[-1]
    local_rows, half_width = atom_rows.shape
    block_count = local_rows // tile_size
    reach_blocks = max(block_count // 2, 1)
    padded = extended(atom_rows, (("atoms", 0),), reach_blocks * tile_size)
    blocks = padded.reshape(block_count + 2 * reach_blocks, tile_size, half_width)
    first_block = lax.axis_index("atoms") * block_count
    row_ids = tile_pair[0]
    col_ids = tile_pair[1]
    live_tiles = row_ids >= 0
    col_local = jnp.where(live_tiles, col_ids - first_block + reach_blocks, 0)
    row_local = jnp.where(live_tiles, row_ids - first_block, -1)
    panels = jnp.take(blocks, col_local, axis=0)
    selector = row_local[None, :] == jnp.arange(block_count, dtype=jnp.int32)[:, None]
    masked = jnp.where(selector[:, :, None, None], tile_block[None], jnp.zeros_like(tile_block[None]))
    summed = jnp.einsum("btij,tjf->bif", masked, panels, preferred_element_type=jnp.float32)
    return summed.reshape(local_rows, half_width).astype(jnp.bfloat16)


def key_summary(key_rows, value_rows, atom_mask, head_count):
    count_rows = key_rows.shape[0]
    feat_keys = (
        feature_map(key_rows.astype(jnp.float32)).reshape(count_rows, head_count, -1)
        * atom_mask[:, None, None]
    )
    value_f = value_rows.astype(jnp.float32).reshape(count_rows, head_count, -1)
    outer_state = jnp.einsum("nhd,nhe->hde", feat_keys, value_f, precision=HIGHEST)
    return (outer_state, jnp.sum(feat_keys, axis=0))


def read_summary(query_rows, outer_state, key_total, head_count):
    count_rows = query_rows.shape[0]
    feat_query = feature_map(query_rows.astype(jnp.float32)).reshape(count_rows, head_count, -1)
    numerator = jnp.einsum("nhd,hde->nhe", feat_query, outer_state, precision=HIGHEST)
    denominator = jnp.einsum("nhd,hd->nh", feat_query, key_total, precision=HIGHEST)
    return (numerator / denominator[..., None]).reshape(count_rows, -1)


def contrast(unit_rows, peak_rows, label_part, mask_part, peak_start):
    logit_scale = 2.0 / math.sqrt(unit_rows.shape[-1])
    peak_f = peak_rows.astype(jnp.float32)
    logits = logit_scale * jnp.dot(unit_rows, peak_f.T, precision=HIGHEST)
    peak_index = peak_start + jnp.arange(peak_rows.shape[0], dtype=jnp.int32)
    target = (label_part[:, None] == peak_index[None, :]).astype(jnp.float32)
    sign_rows = 2.0 * target - 1.0
    loss_part = jnp.sum(mask_part[:, None] * jax.nn.softplus(-sign_rows * logits)) / PEAKS
    slopes = mask_part[:, None] * (jax.nn.sigmoid(logits) - target) * (1.0 / math.sqrt(PEAKS))
    unit_grad = logit_scale * jnp.dot(slopes, peak_f, precision=HIGHEST)
    return (loss_part, unit_grad)


def embed_backward(unit_rows, unit_grad, embed_scale):
    inner_mean = jnp.mean(unit_grad * unit_rows, axis=-1, keepdims=True)
    return (embed_scale * (unit_grad - unit_rows * inner_mean)).astype(jnp.bfloat16)


def shards(
    atoms_in,
    tile_ids,
    tile_vals,
    seq_lens,
    pair_labels,
    peak_embed,
    norm_gain,
    w_query,
    w_key,
    w_value,
    w_out,
    w_proj,
):
    atom_rows = atoms_in[0]
    local_rows = atom_rows.shape[0]
    gathered = message_pass(atom_rows, tile_ids[0], tile_vals[0])
    hidden_one = (atom_rows.astype(jnp.float32) + gathered.astype(jnp.float32)).astype(jnp.bfloat16)
    atom_base = lax.axis_index("atoms") * local_rows
    length_one = seq_lens[0]
    label_row = pair_labels[0]
    peak_part = peak_embed[0]
    hidden_f = hidden_one.astype(jnp.float32)
    square_sum = lax.psum(jnp.sum(hidden_f * hidden_f, axis=-1), "sec")
    row_scale = lax.rsqrt(square_sum[:, None] / D + EPSILON)
    normed = (hidden_f * row_scale * norm_gain.astype(jnp.float32)).astype(jnp.bfloat16)
    head_cols = w_query.shape[1]
    sec = lax.axis_index("sec")
    width = normed.shape[1]
    other_rows = swap_sec(normed)
    out_cols = w_out.reshape(w_out.shape[0], 2, width)
    partner = (swap_sec(peak_part), swap_sec(out_cols[:, 1 - sec, :]))

    def project(weight):
        halves = weight.reshape(2, width, weight.shape[1])
        mine = jnp.dot(normed, halves[sec], preferred_element_type=jnp.float32)
        return mine + jnp.dot(other_rows, halves[1 - sec], preferred_element_type=jnp.float32)

    query_f, key_f, value_f = tuple((project(weight) for weight in (w_query, w_key, w_value)))
    head_count = head_cols // HEAD_DIM
    atom_mask = (atom_base + jnp.arange(local_rows, dtype=jnp.int32) < length_one).astype(
        jnp.float32
    )
    outer_state, key_total = key_summary(
        key_f.astype(jnp.bfloat16), value_f.astype(jnp.bfloat16), atom_mask, head_count
    )
    state_rows = jnp.concatenate([outer_state, key_total[:, None, :]], axis=1)
    packed, partner = sum_atoms(state_rows, riders=partner)
    peak_all = join_sec(peak_part, partner[0], sec, 0)
    out_rows = join_sec(out_cols[:, sec, :], partner[1], sec, 0)
    outer_state, key_total = packed[:, :HEAD_DIM, :], packed[:, HEAD_DIM, :]
    attended = read_summary(query_f.astype(jnp.bfloat16), outer_state, key_total, head_count)
    attended_all = join_sec(attended, swap_sec(attended), sec, 1)
    out_sum = jnp.sum(attended_all * attended_all, axis=-1)
    attended_n = (attended_all * lax.rsqrt(out_sum[:, None] / (HEADS * HEAD_DIM) + EPSILON)).astype(
        jnp.bfloat16
    )
    branch = jnp.dot(attended_n, out_rows, preferred_element_type=jnp.float32)
    hidden_two = (hidden_f + branch).astype(jnp.bfloat16)
    embedded = sum_sec(jnp.dot(hidden_two, w_proj, preferred_element_type=jnp.float32))
    embed_scale = lax.rsqrt(jnp.mean(embedded * embedded, axis=-1, keepdims=True) + EPSILON)
    unit_rows = embedded * embed_scale
    loss_part, unit_grad = contrast(unit_rows, peak_all, label_row, atom_mask, 0)
    embed_grad = embed_backward(unit_rows, unit_grad, embed_scale)
    proj_part = jnp.einsum("nd,ne->de", hidden_two, embed_grad, preferred_element_type=jnp.float32)
    zero = jnp.zeros((1,), jnp.float32)
    payload = jnp.concatenate([proj_part.reshape(-1), loss_part.reshape(1), zero])
    packed = sum_atoms(payload, exact=proj_part.size)
    proj_total = packed[: proj_part.size].reshape(proj_part.shape)
    loss_sum = packed[proj_part.size] + packed[proj_part.size + 1]
    loss_total = loss_sum / (local_rows * lax.axis_size("atoms"))
    return (hidden_two[None], loss_total.reshape(1), proj_total[None])


def solution(mesh):
    return jax.shard_map(
        shards,
        mesh=mesh,
        in_specs=(
            P("batch", "atoms", "sec"),
            P("batch", None, "atoms"),
            P("batch", "atoms", None, None),
            P("batch"),
            P("batch", "atoms"),
            P("batch", "sec", None),
            P("sec"),
            P(None, "sec"),
            P(None, "sec"),
            P(None, "sec"),
            P("sec", None),
            P("sec", None),
        ),
        out_specs=(P("batch", "atoms", "sec"), P("batch"), P("batch", "sec", None)),
        check_vma=False,
    )
```

```python
import math

import jax
import jax.numpy as jnp
from jax import lax
from jax.sharding import PartitionSpec as P

D = 1024
HEADS = 8
HEAD_DIM = 64
PEAKS = 256


EPSILON = 1e-06
HIGHEST = lax.Precision.HIGHEST


def extended(x, sides, width):
    for axis, dim in sides:
        peers, length = (lax.axis_size(axis), x.shape[dim])
        up = [(i, (i + 1) % peers) for i in range(peers - 1)]
        down = [(j, i) for i, j in up]
        last = lax.slice_in_dim(x, length - width, length, axis=dim)
        leading = lax.slice_in_dim(x, 0, width, axis=dim)
        before = lax.ppermute(last, axis, up)
        after = lax.ppermute(leading, axis, down)
        x = jnp.concatenate([before, x, after], axis=dim)
    return x


def swap_sec(x):
    return lax.ppermute(x, "sec", [(0, 1), (1, 0)])


def join_sec(mine, other, sec, axis):
    first = jnp.where(sec == 0, mine, other)
    second = jnp.where(sec == 0, other, mine)
    return jnp.concatenate([first, second], axis=axis)


def sum_atoms(x, exact=None, riders=None):
    peers = lax.axis_size("atoms")
    flat = x.reshape(-1)
    chunk = -(-flat.shape[0] // (peers * 128)) * 128
    flat = jnp.pad(flat, (0, chunk * peers - flat.shape[0]))
    pieces = flat.reshape(peers, chunk // 128, 128)
    arrived = lax.all_to_all(pieces, "atoms", 0, 0, tiled=True)
    if riders is not None:
        arrived, riders = lax.optimization_barrier((arrived, riders))
    owned = jnp.sum(arrived, axis=0, keepdims=True)
    if exact is not None:
        owner, slot = divmod(exact, chunk)
        rest = owned - owned.astype(jnp.bfloat16).astype(jnp.float32)
        here = lax.axis_index("atoms") == owner
        spare = (slot + 1) // 128, (slot + 1) % 128
        kept = jnp.where(here, rest[0, slot // 128, slot % 128], owned[0, spare[0], spare[1]])
        owned = owned.at[0, spare[0], spare[1]].set(kept).astype(jnp.bfloat16)
    spread = lax.all_to_all(jnp.broadcast_to(owned, pieces.shape), "atoms", 0, 0, tiled=True)
    total = spread.reshape(-1)[: x.size].reshape(x.shape).astype(jnp.float32)
    return total if riders is None else (total, riders)


def feature_map(values):
    return jax.nn.elu(values) + 1.0


def message_pass(atom_rows, tile_pair, tile_block):
    tile_size = tile_block.shape[-1]
    local_rows, half_width = atom_rows.shape
    block_count = local_rows // tile_size
    reach_blocks = max(block_count // 2, 1)
    padded = extended(atom_rows, (("atoms", 0),), reach_blocks * tile_size)
    blocks = padded.reshape(block_count + 2 * reach_blocks, tile_size, half_width)
    first_block = lax.axis_index("atoms") * block_count
    row_ids = tile_pair[0]
    col_ids = tile_pair[1]
    live_tiles = row_ids >= 0
    col_local = jnp.where(live_tiles, col_ids - first_block + reach_blocks, 0)
    row_local = jnp.where(live_tiles, row_ids - first_block, -1)
    panels = jnp.take(blocks, col_local, axis=0)
    selector = row_local[None, :] == jnp.arange(block_count, dtype=jnp.int32)[:, None]
    masked = jnp.where(selector[:, :, None, None], tile_block[None], jnp.zeros_like(tile_block[None]))
    summed = jnp.einsum("btij,tjf->bif", masked, panels, preferred_element_type=jnp.float32)
    return summed.reshape(local_rows, half_width).astype(jnp.bfloat16)


def key_summary(key_rows, value_rows, atom_mask, head_count):
    count_rows = key_rows.shape[0]
    feat_keys = (
        feature_map(key_rows.astype(jnp.float32)).reshape(count_rows, head_count, -1)
        * atom_mask[:, None, None]
    )
    value_f = value_rows.astype(jnp.float32).reshape(count_rows, head_count, -1)
    outer_state = jnp.einsum("nhd,nhe->hde", feat_keys, value_f, precision=HIGHEST)
    return (outer_state, jnp.sum(feat_keys, axis=0))


def read_summary(query_rows, outer_state, key_total, head_count):
    count_rows = query_rows.shape[0]
    feat_query = feature_map(query_rows.astype(jnp.float32)).reshape(count_rows, head_count, -1)
    numerator = jnp.einsum("nhd,hde->nhe", feat_query, outer_state, precision=HIGHEST)
    denominator = jnp.einsum("nhd,hd->nh", feat_query, key_total, precision=HIGHEST)
    return (numerator / denominator[..., None]).reshape(count_rows, -1)


def contrast(unit_rows, peak_rows, label_part, mask_part, peak_start):
    logit_scale = 2.0 / math.sqrt(unit_rows.shape[-1])
    peak_f = peak_rows.astype(jnp.float32)
    logits = logit_scale * jnp.dot(unit_rows, peak_f.T, precision=HIGHEST)
    peak_index = peak_start + jnp.arange(peak_rows.shape[0], dtype=jnp.int32)
    target = (label_part[:, None] == peak_index[None, :]).astype(jnp.float32)
    sign_rows = 2.0 * target - 1.0
    loss_part = jnp.sum(mask_part[:, None] * jax.nn.softplus(-sign_rows * logits)) / PEAKS
    slopes = mask_part[:, None] * (jax.nn.sigmoid(logits) - target) * (1.0 / math.sqrt(PEAKS))
    unit_grad = logit_scale * jnp.dot(slopes, peak_f, precision=HIGHEST)
    return (loss_part, unit_grad)


def embed_backward(unit_rows, unit_grad, embed_scale):
    inner_mean = jnp.mean(unit_grad * unit_rows, axis=-1, keepdims=True)
    return (embed_scale * (unit_grad - unit_rows * inner_mean)).astype(jnp.bfloat16)


def shards(
    atoms_in,
    tile_ids,
    tile_vals,
    seq_lens,
    pair_labels,
    peak_embed,
    norm_gain,
    w_query,
    w_key,
    w_value,
    w_out,
    w_proj,
):
    atom_rows = atoms_in[0]
    local_rows, width = atom_rows.shape
    sec = lax.axis_index("sec")
    peak_part = peak_embed[0]
    peak_count, embed_width = peak_part.shape
    early = swap_sec(jnp.concatenate([peak_part, norm_gain.reshape(-1, embed_width)], axis=0))
    peak_other, gain_other = early[:peak_count], early[peak_count:].reshape(-1)
    partner = (swap_sec(w_out), swap_sec(w_proj))
    gathered = message_pass(atom_rows, tile_ids[0], tile_vals[0])
    hidden_one = (atom_rows.astype(jnp.float32) + gathered.astype(jnp.float32)).astype(jnp.bfloat16)
    mine_f = hidden_one.astype(jnp.float32)
    other_f = swap_sec(hidden_one).astype(jnp.float32)
    atom_base = lax.axis_index("atoms") * local_rows
    length_one = seq_lens[0]
    label_row = pair_labels[0]
    square_sum = jnp.sum(mine_f * mine_f, axis=-1, keepdims=True) + jnp.sum(
        other_f * other_f, axis=-1, keepdims=True
    )
    row_scale = lax.rsqrt(square_sum / D + EPSILON)
    normed_mine = (mine_f * row_scale * norm_gain.astype(jnp.float32)).astype(jnp.bfloat16)
    normed_other = (other_f * row_scale * gain_other.astype(jnp.float32)).astype(jnp.bfloat16)
    head_cols = w_query.shape[1]

    def project(weight):
        halves = weight.reshape(2, width, weight.shape[1])
        mine = jnp.dot(normed_mine, halves[sec], preferred_element_type=jnp.float32)
        return mine + jnp.dot(normed_other, halves[1 - sec], preferred_element_type=jnp.float32)

    query_f, key_f, value_f = tuple((project(weight) for weight in (w_query, w_key, w_value)))
    head_count = head_cols // HEAD_DIM
    atom_mask = (atom_base + jnp.arange(local_rows, dtype=jnp.int32) < length_one).astype(
        jnp.float32
    )
    outer_state, key_total = key_summary(
        key_f.astype(jnp.bfloat16), value_f.astype(jnp.bfloat16), atom_mask, head_count
    )
    state_rows = jnp.concatenate([outer_state, key_total[:, None, :]], axis=1)
    packed, partner = sum_atoms(state_rows, riders=partner)
    out_other, proj_other = partner
    outer_state, key_total = packed[:, :HEAD_DIM, :], packed[:, HEAD_DIM, :]
    attended = read_summary(query_f.astype(jnp.bfloat16), outer_state, key_total, head_count)
    attended_other = swap_sec(attended)
    out_sum = jnp.sum(attended * attended, axis=-1, keepdims=True) + jnp.sum(
        attended_other * attended_other, axis=-1, keepdims=True
    )
    out_scale = lax.rsqrt(out_sum / (HEADS * HEAD_DIM) + EPSILON)
    normed_att = (attended * out_scale).astype(jnp.bfloat16)
    normed_att_other = (attended_other * out_scale).astype(jnp.bfloat16)
    out_mine = w_out.reshape(w_out.shape[0], 2, width)
    out_other = out_other.reshape(out_mine.shape)

    def branch_for(half):
        return jnp.dot(normed_att, out_mine[:, half, :], preferred_element_type=jnp.float32) + jnp.dot(
            normed_att_other, out_other[:, half, :], preferred_element_type=jnp.float32
        )

    hidden_two = (mine_f + branch_for(sec)).astype(jnp.bfloat16)
    hidden_other = (other_f + branch_for(1 - sec)).astype(jnp.bfloat16)
    embedded = jnp.dot(hidden_two, w_proj, preferred_element_type=jnp.float32) + jnp.dot(
        hidden_other, proj_other, preferred_element_type=jnp.float32
    )
    embed_scale = lax.rsqrt(jnp.mean(embedded * embedded, axis=-1, keepdims=True) + EPSILON)
    unit_rows = embedded * embed_scale
    peak_all = join_sec(peak_part, peak_other, sec, 0)
    loss_part, unit_grad = contrast(unit_rows, peak_all, label_row, atom_mask, 0)
    embed_grad = embed_backward(unit_rows, unit_grad, embed_scale)
    proj_part = jnp.einsum("nd,ne->de", hidden_two, embed_grad, preferred_element_type=jnp.float32)
    zero = jnp.zeros((1,), jnp.float32)
    payload = jnp.concatenate([proj_part.reshape(-1), loss_part.reshape(1), zero])
    packed = sum_atoms(payload, exact=proj_part.size)
    proj_total = packed[: proj_part.size].reshape(proj_part.shape)
    loss_sum = packed[proj_part.size] + packed[proj_part.size + 1]
    loss_total = loss_sum / (local_rows * lax.axis_size("atoms"))
    return (hidden_two[None], loss_total.reshape(1), proj_total[None])


def solution(mesh):
    return jax.shard_map(
        shards,
        mesh=mesh,
        in_specs=(
            P("batch", "atoms", "sec"),
            P("batch", None, "atoms"),
            P("batch", "atoms", None, None),
            P("batch"),
            P("batch", "atoms"),
            P("batch", "sec", None),
            P("sec"),
            P(None, "sec"),
            P(None, "sec"),
            P(None, "sec"),
            P("sec", None),
            P("sec", None),
        ),
        out_specs=(P("batch", "atoms", "sec"), P("batch"), P("batch", "sec", None)),
        check_vma=False,
    )
```

```python
import math

import jax
import jax.numpy as jnp
from jax import lax
from jax.sharding import PartitionSpec as P

D = 1024
HEADS = 8
HEAD_DIM = 64
PEAKS = 256


EPSILON = 1e-06
HIGHEST = lax.Precision.HIGHEST


def extended(x, sides, width):
    for axis, dim in sides:
        peers, length = (lax.axis_size(axis), x.shape[dim])
        up = [(i, (i + 1) % peers) for i in range(peers - 1)]
        down = [(j, i) for i, j in up]
        last = lax.slice_in_dim(x, length - width, length, axis=dim)
        leading = lax.slice_in_dim(x, 0, width, axis=dim)
        before = lax.ppermute(last, axis, up)
        after = lax.ppermute(leading, axis, down)
        x = jnp.concatenate([before, x, after], axis=dim)
    return x


def swap_sec(x):
    return lax.ppermute(x, "sec", [(0, 1), (1, 0)])


def join_sec(mine, other, sec, axis):
    first = jnp.where(sec == 0, mine, other)
    second = jnp.where(sec == 0, other, mine)
    return jnp.concatenate([first, second], axis=axis)


def sum_sec(x):
    return x + swap_sec(x)


def sum_atoms(x, exact=None, riders=None):
    peers = lax.axis_size("atoms")
    flat = x.reshape(-1)
    chunk = -(-flat.shape[0] // (peers * 128)) * 128
    flat = jnp.pad(flat, (0, chunk * peers - flat.shape[0]))
    pieces = flat.reshape(peers, chunk // 128, 128)
    arrived = lax.all_to_all(pieces, "atoms", 0, 0, tiled=True)
    if riders is not None:
        arrived, riders = lax.optimization_barrier((arrived, riders))
    owned = jnp.sum(arrived, axis=0, keepdims=True)
    if exact is not None:
        owner, slot = divmod(exact, chunk)
        rest = owned - owned.astype(jnp.bfloat16).astype(jnp.float32)
        here = lax.axis_index("atoms") == owner
        spare = (slot + 1) // 128, (slot + 1) % 128
        kept = jnp.where(here, rest[0, slot // 128, slot % 128], owned[0, spare[0], spare[1]])
        owned = owned.at[0, spare[0], spare[1]].set(kept).astype(jnp.bfloat16)
    spread = lax.all_to_all(jnp.broadcast_to(owned, pieces.shape), "atoms", 0, 0, tiled=True)
    total = spread.reshape(-1)[: x.size].reshape(x.shape).astype(jnp.float32)
    return total if riders is None else (total, riders)


def feature_map(values):
    return jax.nn.elu(values) + 1.0


def message_pass(atom_rows, tile_pair, tile_block):
    tile_size = tile_block.shape[-1]
    local_rows, half_width = atom_rows.shape
    block_count = local_rows // tile_size
    reach_blocks = max(block_count // 2, 1)
    padded = extended(atom_rows, (("atoms", 0),), reach_blocks * tile_size)
    blocks = padded.reshape(block_count + 2 * reach_blocks, tile_size, half_width)
    first_block = lax.axis_index("atoms") * block_count
    row_ids = tile_pair[0]
    col_ids = tile_pair[1]
    live_tiles = row_ids >= 0
    col_local = jnp.where(live_tiles, col_ids - first_block + reach_blocks, 0)
    row_local = jnp.where(live_tiles, row_ids - first_block, -1)
    panels = jnp.take(blocks, col_local, axis=0)
    selector = row_local[None, :] == jnp.arange(block_count, dtype=jnp.int32)[:, None]
    masked = jnp.where(selector[:, :, None, None], tile_block[None], jnp.zeros_like(tile_block[None]))
    summed = jnp.einsum("btij,tjf->bif", masked, panels, preferred_element_type=jnp.float32)
    return summed.reshape(local_rows, half_width).astype(jnp.bfloat16)


def key_summary(key_rows, value_rows, atom_mask, head_count):
    count_rows = key_rows.shape[0]
    feat_keys = (
        feature_map(key_rows.astype(jnp.float32)).reshape(count_rows, head_count, -1)
        * atom_mask[:, None, None]
    )
    value_f = value_rows.astype(jnp.float32).reshape(count_rows, head_count, -1)
    outer_state = jnp.einsum("nhd,nhe->hde", feat_keys, value_f, precision=HIGHEST)
    return (outer_state, jnp.sum(feat_keys, axis=0))


def read_summary(query_rows, outer_state, key_total, head_count):
    count_rows = query_rows.shape[0]
    feat_query = feature_map(query_rows.astype(jnp.float32)).reshape(count_rows, head_count, -1)
    numerator = jnp.einsum("nhd,hde->nhe", feat_query, outer_state, precision=HIGHEST)
    denominator = jnp.einsum("nhd,hd->nh", feat_query, key_total, precision=HIGHEST)
    return (numerator / denominator[..., None]).reshape(count_rows, -1)


def contrast(unit_rows, peak_rows, label_part, mask_part, peak_start):
    logit_scale = 2.0 / math.sqrt(unit_rows.shape[-1])
    peak_f = peak_rows.astype(jnp.float32)
    logits = logit_scale * jnp.dot(unit_rows, peak_f.T, precision=HIGHEST)
    peak_index = peak_start + jnp.arange(peak_rows.shape[0], dtype=jnp.int32)
    target = (label_part[:, None] == peak_index[None, :]).astype(jnp.float32)
    sign_rows = 2.0 * target - 1.0
    loss_part = jnp.sum(mask_part[:, None] * jax.nn.softplus(-sign_rows * logits)) / PEAKS
    slopes = mask_part[:, None] * (jax.nn.sigmoid(logits) - target) * (1.0 / math.sqrt(PEAKS))
    unit_grad = logit_scale * jnp.dot(slopes, peak_f, precision=HIGHEST)
    return (loss_part, unit_grad)


def embed_backward(unit_rows, unit_grad, embed_scale):
    inner_mean = jnp.mean(unit_grad * unit_rows, axis=-1, keepdims=True)
    return (embed_scale * (unit_grad - unit_rows * inner_mean)).astype(jnp.bfloat16)


def shards(
    atoms_in,
    tile_ids,
    tile_vals,
    seq_lens,
    pair_labels,
    peak_embed,
    norm_gain,
    w_query,
    w_key,
    w_value,
    w_out,
    w_proj,
):
    atom_rows = atoms_in[0]
    local_rows = atom_rows.shape[0]
    sec = lax.axis_index("sec")
    peak_part = peak_embed[0]
    peak_count, embed_width = peak_part.shape
    early = swap_sec(jnp.concatenate([peak_part, norm_gain.reshape(-1, embed_width)], axis=0))
    peak_other, gain_other = early[:peak_count], early[peak_count:].reshape(-1)
    gathered = message_pass(atom_rows, tile_ids[0], tile_vals[0])
    hidden_one = (atom_rows.astype(jnp.float32) + gathered.astype(jnp.float32)).astype(jnp.bfloat16)
    atom_base = lax.axis_index("atoms") * local_rows
    length_one = seq_lens[0]
    label_row = pair_labels[0]
    hidden_f = hidden_one.astype(jnp.float32)
    other_f = swap_sec(hidden_one).astype(jnp.float32)
    square_sum = jnp.sum(hidden_f * hidden_f, axis=-1, keepdims=True) + jnp.sum(
        other_f * other_f, axis=-1, keepdims=True
    )
    row_scale = lax.rsqrt(square_sum / D + EPSILON)
    normed = (hidden_f * row_scale * norm_gain.astype(jnp.float32)).astype(jnp.bfloat16)
    other_rows = (other_f * row_scale * gain_other.astype(jnp.float32)).astype(jnp.bfloat16)
    head_cols = w_query.shape[1]
    width = normed.shape[1]
    out_cols = w_out.reshape(w_out.shape[0], 2, width)
    partner = swap_sec(out_cols[:, 1 - sec, :])

    def project(weight):
        halves = weight.reshape(2, width, weight.shape[1])
        mine = jnp.dot(normed, halves[sec], preferred_element_type=jnp.float32)
        return mine + jnp.dot(other_rows, halves[1 - sec], preferred_element_type=jnp.float32)

    query_f, key_f, value_f = tuple((project(weight) for weight in (w_query, w_key, w_value)))
    head_count = head_cols // HEAD_DIM
    atom_mask = (atom_base + jnp.arange(local_rows, dtype=jnp.int32) < length_one).astype(
        jnp.float32
    )
    outer_state, key_total = key_summary(
        key_f.astype(jnp.bfloat16), value_f.astype(jnp.bfloat16), atom_mask, head_count
    )
    state_rows = jnp.concatenate([outer_state, key_total[:, None, :]], axis=1)
    packed, partner = sum_atoms(state_rows, riders=partner)
    peak_all = join_sec(peak_part, peak_other, sec, 0)
    out_rows = join_sec(out_cols[:, sec, :], partner, sec, 0)
    outer_state, key_total = packed[:, :HEAD_DIM, :], packed[:, HEAD_DIM, :]
    attended = read_summary(query_f.astype(jnp.bfloat16), outer_state, key_total, head_count)
    attended_all = join_sec(attended, swap_sec(attended), sec, 1)
    out_sum = jnp.sum(attended_all * attended_all, axis=-1)
    attended_n = (attended_all * lax.rsqrt(out_sum[:, None] / (HEADS * HEAD_DIM) + EPSILON)).astype(
        jnp.bfloat16
    )
    branch = jnp.dot(attended_n, out_rows, preferred_element_type=jnp.float32)
    hidden_two = (hidden_f + branch).astype(jnp.bfloat16)
    embedded = sum_sec(jnp.dot(hidden_two, w_proj, preferred_element_type=jnp.float32))
    embed_scale = lax.rsqrt(jnp.mean(embedded * embedded, axis=-1, keepdims=True) + EPSILON)
    unit_rows = embedded * embed_scale
    loss_part, unit_grad = contrast(unit_rows, peak_all, label_row, atom_mask, 0)
    embed_grad = embed_backward(unit_rows, unit_grad, embed_scale)
    proj_part = jnp.einsum("nd,ne->de", hidden_two, embed_grad, preferred_element_type=jnp.float32)
    zero = jnp.zeros((1,), jnp.float32)
    payload = jnp.concatenate([proj_part.reshape(-1), loss_part.reshape(1), zero])
    packed = sum_atoms(payload, exact=proj_part.size)
    proj_total = packed[: proj_part.size].reshape(proj_part.shape)
    loss_sum = packed[proj_part.size] + packed[proj_part.size + 1]
    loss_total = loss_sum / (local_rows * lax.axis_size("atoms"))
    return (hidden_two[None], loss_total.reshape(1), proj_total[None])


def solution(mesh):
    return jax.shard_map(
        shards,
        mesh=mesh,
        in_specs=(
            P("batch", "atoms", "sec"),
            P("batch", None, "atoms"),
            P("batch", "atoms", None, None),
            P("batch"),
            P("batch", "atoms"),
            P("batch", "sec", None),
            P("sec"),
            P(None, "sec"),
            P(None, "sec"),
            P(None, "sec"),
            P("sec", None),
            P("sec", None),
        ),
        out_specs=(P("batch", "atoms", "sec"), P("batch"), P("batch", "sec", None)),
        check_vma=False,
    )
```

```python
import math

import jax
import jax.numpy as jnp
from jax import lax
from jax.sharding import PartitionSpec as P

D = 1024
HEADS = 8
HEAD_DIM = 64
PEAKS = 256


EPSILON = 1e-06
HIGHEST = lax.Precision.HIGHEST


def extended(x, sides, width):
    for axis, dim in sides:
        peers, length = (lax.axis_size(axis), x.shape[dim])
        up = [(i, (i + 1) % peers) for i in range(peers - 1)]
        down = [(j, i) for i, j in up]
        last = lax.slice_in_dim(x, length - width, length, axis=dim)
        leading = lax.slice_in_dim(x, 0, width, axis=dim)
        before = lax.ppermute(last, axis, up)
        after = lax.ppermute(leading, axis, down)
        x = jnp.concatenate([before, x, after], axis=dim)
    return x


def swap_sec(x):
    return lax.ppermute(x, "sec", [(0, 1), (1, 0)])


def join_sec(mine, other, sec, axis):
    first = jnp.where(sec == 0, mine, other)
    second = jnp.where(sec == 0, other, mine)
    return jnp.concatenate([first, second], axis=axis)


def sum_sec(x):
    return x + swap_sec(x)


def sum_atoms(x, exact=None, riders=None):
    peers = lax.axis_size("atoms")
    flat = x.reshape(-1)
    chunk = -(-flat.shape[0] // (peers * 128)) * 128
    flat = jnp.pad(flat, (0, chunk * peers - flat.shape[0]))
    pieces = flat.reshape(peers, chunk // 128, 128)
    arrived = lax.all_to_all(pieces, "atoms", 0, 0, tiled=True)
    if riders is not None:
        arrived, riders = lax.optimization_barrier((arrived, riders))
    owned = jnp.sum(arrived, axis=0, keepdims=True)
    if exact is not None:
        owner, slot = divmod(exact, chunk)
        rest = owned - owned.astype(jnp.bfloat16).astype(jnp.float32)
        here = lax.axis_index("atoms") == owner
        spare = (slot + 1) // 128, (slot + 1) % 128
        kept = jnp.where(here, rest[0, slot // 128, slot % 128], owned[0, spare[0], spare[1]])
        owned = owned.at[0, spare[0], spare[1]].set(kept).astype(jnp.bfloat16)
    spread = lax.all_to_all(jnp.broadcast_to(owned, pieces.shape), "atoms", 0, 0, tiled=True)
    total = spread.reshape(-1)[: x.size].reshape(x.shape).astype(jnp.float32)
    return total if riders is None else (total, riders)


def feature_map(values):
    return jax.nn.elu(values) + 1.0


def message_pass(atom_rows, tile_pair, tile_block):
    tile_size = tile_block.shape[-1]
    local_rows, half_width = atom_rows.shape
    block_count = local_rows // tile_size
    reach_blocks = max(block_count // 2, 1)
    padded = extended(atom_rows, (("atoms", 0),), reach_blocks * tile_size)
    blocks = padded.reshape(block_count + 2 * reach_blocks, tile_size, half_width)
    first_block = lax.axis_index("atoms") * block_count
    row_ids = tile_pair[0]
    col_ids = tile_pair[1]
    live_tiles = row_ids >= 0
    col_local = jnp.where(live_tiles, col_ids - first_block + reach_blocks, 0)
    row_local = jnp.where(live_tiles, row_ids - first_block, -1)
    panels = jnp.take(blocks, col_local, axis=0)
    selector = row_local[None, :] == jnp.arange(block_count, dtype=jnp.int32)[:, None]
    masked = jnp.where(selector[:, :, None, None], tile_block[None], jnp.zeros_like(tile_block[None]))
    summed = jnp.einsum("btij,tjf->bif", masked, panels, preferred_element_type=jnp.float32)
    return summed.reshape(local_rows, half_width).astype(jnp.bfloat16)


def key_summary(key_rows, value_rows, atom_mask, head_count):
    count_rows = key_rows.shape[0]
    feat_keys = (
        feature_map(key_rows.astype(jnp.float32)).reshape(count_rows, head_count, -1)
        * atom_mask[:, None, None]
    )
    value_f = value_rows.astype(jnp.float32).reshape(count_rows, head_count, -1)
    outer_state = jnp.einsum("nhd,nhe->hde", feat_keys, value_f, precision=HIGHEST)
    return (outer_state, jnp.sum(feat_keys, axis=0))


def read_summary(query_rows, outer_state, key_total, head_count):
    count_rows = query_rows.shape[0]
    feat_query = feature_map(query_rows.astype(jnp.float32)).reshape(count_rows, head_count, -1)
    numerator = jnp.einsum("nhd,hde->nhe", feat_query, outer_state, precision=HIGHEST)
    denominator = jnp.einsum("nhd,hd->nh", feat_query, key_total, precision=HIGHEST)
    return (numerator / denominator[..., None]).reshape(count_rows, -1)


def contrast(unit_rows, peak_rows, label_part, mask_part, peak_start):
    logit_scale = 2.0 / math.sqrt(unit_rows.shape[-1])
    peak_f = peak_rows.astype(jnp.float32)
    logits = logit_scale * jnp.dot(unit_rows, peak_f.T, precision=HIGHEST)
    peak_index = peak_start + jnp.arange(peak_rows.shape[0], dtype=jnp.int32)
    target = (label_part[:, None] == peak_index[None, :]).astype(jnp.float32)
    sign_rows = 2.0 * target - 1.0
    loss_part = jnp.sum(mask_part[:, None] * jax.nn.softplus(-sign_rows * logits)) / PEAKS
    slopes = mask_part[:, None] * (jax.nn.sigmoid(logits) - target) * (1.0 / math.sqrt(PEAKS))
    unit_grad = logit_scale * jnp.dot(slopes, peak_f, precision=HIGHEST)
    return (loss_part, unit_grad)


def embed_backward(unit_rows, unit_grad, embed_scale):
    inner_mean = jnp.mean(unit_grad * unit_rows, axis=-1, keepdims=True)
    return (embed_scale * (unit_grad - unit_rows * inner_mean)).astype(jnp.bfloat16)


def shards(
    atoms_in,
    tile_ids,
    tile_vals,
    seq_lens,
    pair_labels,
    peak_embed,
    norm_gain,
    w_query,
    w_key,
    w_value,
    w_out,
    w_proj,
):
    atom_rows = atoms_in[0]
    local_rows = atom_rows.shape[0]
    gathered = message_pass(atom_rows, tile_ids[0], tile_vals[0])
    hidden_one = (atom_rows.astype(jnp.float32) + gathered.astype(jnp.float32)).astype(jnp.bfloat16)
    atom_base = lax.axis_index("atoms") * local_rows
    length_one = seq_lens[0]
    label_row = pair_labels[0]
    peak_part = peak_embed[0]
    hidden_f = hidden_one.astype(jnp.float32)
    square_sum = lax.psum(jnp.sum(hidden_f * hidden_f, axis=-1), "sec")
    row_scale = lax.rsqrt(square_sum[:, None] / D + EPSILON)
    normed = (hidden_f * row_scale * norm_gain.astype(jnp.float32)).astype(jnp.bfloat16)
    head_cols = w_query.shape[1]
    sec = lax.axis_index("sec")
    width = normed.shape[1]
    other_rows = swap_sec(normed)
    out_cols = w_out.reshape(w_out.shape[0], 2, width)
    partner = (swap_sec(peak_part), swap_sec(out_cols[:, 1 - sec, :]))

    def project(weight):
        halves = weight.reshape(2, width, weight.shape[1])
        mine = jnp.dot(normed, halves[sec], preferred_element_type=jnp.float32)
        return mine + jnp.dot(other_rows, halves[1 - sec], preferred_element_type=jnp.float32)

    query_f, key_f, value_f = tuple((project(weight) for weight in (w_query, w_key, w_value)))
    head_count = head_cols // HEAD_DIM
    atom_mask = (atom_base + jnp.arange(local_rows, dtype=jnp.int32) < length_one).astype(
        jnp.float32
    )
    outer_state, key_total = key_summary(
        key_f.astype(jnp.bfloat16), value_f.astype(jnp.bfloat16), atom_mask, head_count
    )
    state_rows = jnp.concatenate([outer_state, key_total[:, None, :]], axis=1)
    packed, partner = sum_atoms(state_rows, riders=partner)
    peak_all = join_sec(peak_part, partner[0], sec, 0)
    outer_state, key_total = packed[:, :HEAD_DIM, :], packed[:, HEAD_DIM, :]
    attended = read_summary(query_f.astype(jnp.bfloat16), outer_state, key_total, head_count)
    attended_other = swap_sec(attended)
    out_sum = jnp.sum(attended * attended, axis=-1, keepdims=True) + jnp.sum(
        attended_other * attended_other, axis=-1, keepdims=True
    )
    out_scale = lax.rsqrt(out_sum / (HEADS * HEAD_DIM) + EPSILON)
    branch = jnp.dot(
        (attended * out_scale).astype(jnp.bfloat16), out_cols[:, sec, :], preferred_element_type=jnp.float32
    ) + jnp.dot(
        (attended_other * out_scale).astype(jnp.bfloat16), partner[1], preferred_element_type=jnp.float32
    )
    hidden_two = (hidden_f + branch).astype(jnp.bfloat16)
    embedded = sum_sec(jnp.dot(hidden_two, w_proj, preferred_element_type=jnp.float32))
    embed_scale = lax.rsqrt(jnp.mean(embedded * embedded, axis=-1, keepdims=True) + EPSILON)
    unit_rows = embedded * embed_scale
    loss_part, unit_grad = contrast(unit_rows, peak_all, label_row, atom_mask, 0)
    embed_grad = embed_backward(unit_rows, unit_grad, embed_scale)
    proj_part = jnp.einsum("nd,ne->de", hidden_two, embed_grad, preferred_element_type=jnp.float32)
    zero = jnp.zeros((1,), jnp.float32)
    payload = jnp.concatenate([proj_part.reshape(-1), loss_part.reshape(1), zero])
    packed = sum_atoms(payload, exact=proj_part.size)
    proj_total = packed[: proj_part.size].reshape(proj_part.shape)
    loss_sum = packed[proj_part.size] + packed[proj_part.size + 1]
    loss_total = loss_sum / (local_rows * lax.axis_size("atoms"))
    return (hidden_two[None], loss_total.reshape(1), proj_total[None])


def solution(mesh):
    return jax.shard_map(
        shards,
        mesh=mesh,
        in_specs=(
            P("batch", "atoms", "sec"),
            P("batch", None, "atoms"),
            P("batch", "atoms", None, None),
            P("batch"),
            P("batch", "atoms"),
            P("batch", "sec", None),
            P("sec"),
            P(None, "sec"),
            P(None, "sec"),
            P(None, "sec"),
            P("sec", None),
            P("sec", None),
        ),
        out_specs=(P("batch", "atoms", "sec"), P("batch"), P("batch", "sec", None)),
        check_vma=False,
    )
```

```python
import math

import jax
import jax.numpy as jnp
from jax import lax
from jax.sharding import PartitionSpec as P

D = 1024
HEADS = 8
HEAD_DIM = 64
PEAKS = 256


EPSILON = 1e-06
HIGHEST = lax.Precision.HIGHEST


def extended(x, sides, width):
    for axis, dim in sides:
        peers, length = (lax.axis_size(axis), x.shape[dim])
        up = [(i, (i + 1) % peers) for i in range(peers - 1)]
        down = [(j, i) for i, j in up]
        last = lax.slice_in_dim(x, length - width, length, axis=dim)
        leading = lax.slice_in_dim(x, 0, width, axis=dim)
        before = lax.ppermute(last, axis, up)
        after = lax.ppermute(leading, axis, down)
        x = jnp.concatenate([before, x, after], axis=dim)
    return x


def swap_sec(x):
    return lax.ppermute(x, "sec", [(0, 1), (1, 0)])


def join_sec(mine, other, sec, axis):
    first = jnp.where(sec == 0, mine, other)
    second = jnp.where(sec == 0, other, mine)
    return jnp.concatenate([first, second], axis=axis)


def sum_sec(x):
    return x + swap_sec(x)


def sum_atoms(x, exact=None, riders=None):
    peers = lax.axis_size("atoms")
    flat = x.reshape(-1)
    chunk = -(-flat.shape[0] // (peers * 128)) * 128
    flat = jnp.pad(flat, (0, chunk * peers - flat.shape[0]))
    pieces = flat.reshape(peers, chunk // 128, 128)
    arrived = lax.all_to_all(pieces, "atoms", 0, 0, tiled=True)
    if riders is not None:
        arrived, riders = lax.optimization_barrier((arrived, riders))
    owned = jnp.sum(arrived, axis=0, keepdims=True)
    if exact is not None:
        owner, slot = divmod(exact, chunk)
        rest = owned - owned.astype(jnp.bfloat16).astype(jnp.float32)
        here = lax.axis_index("atoms") == owner
        spare = (slot + 1) // 128, (slot + 1) % 128
        row = lax.broadcasted_iota(jnp.int32, owned.shape, 1)
        lane = lax.broadcasted_iota(jnp.int32, owned.shape, 2)
        target = here & (row == spare[0]) & (lane == spare[1])
        owned = jnp.where(target, rest[0, slot // 128, slot % 128], owned).astype(jnp.bfloat16)
    spread = lax.all_to_all(jnp.broadcast_to(owned, pieces.shape), "atoms", 0, 0, tiled=True)
    total = spread.reshape(-1)[: x.size].reshape(x.shape).astype(jnp.float32)
    return total if riders is None else (total, riders)


def feature_map(values):
    return jax.nn.elu(values) + 1.0


def message_pass(atom_rows, tile_pair, tile_block):
    tile_size = tile_block.shape[-1]
    local_rows, half_width = atom_rows.shape
    block_count = local_rows // tile_size
    reach_blocks = max(block_count // 2, 1)
    padded = extended(atom_rows, (("atoms", 0),), reach_blocks * tile_size)
    blocks = padded.reshape(block_count + 2 * reach_blocks, tile_size, half_width)
    first_block = lax.axis_index("atoms") * block_count
    row_ids = tile_pair[0]
    col_ids = tile_pair[1]
    live_tiles = row_ids >= 0
    col_local = jnp.where(live_tiles, col_ids - first_block + reach_blocks, 0)
    row_local = jnp.where(live_tiles, row_ids - first_block, -1)
    panels = jnp.take(blocks, col_local, axis=0)
    selector = row_local[None, :] == jnp.arange(block_count, dtype=jnp.int32)[:, None]
    masked = jnp.where(selector[:, :, None, None], tile_block[None], jnp.zeros_like(tile_block[None]))
    summed = jnp.einsum("btij,tjf->bif", masked, panels, preferred_element_type=jnp.float32)
    return summed.reshape(local_rows, half_width).astype(jnp.bfloat16)


def key_summary(key_rows, value_rows, atom_mask, head_count):
    count_rows = key_rows.shape[0]
    feat_keys = (
        feature_map(key_rows.astype(jnp.float32)).reshape(count_rows, head_count, -1)
        * atom_mask[:, None, None]
    )
    value_f = value_rows.astype(jnp.float32).reshape(count_rows, head_count, -1)
    outer_state = jnp.einsum("nhd,nhe->hde", feat_keys, value_f, precision=HIGHEST)
    return (outer_state, jnp.sum(feat_keys, axis=0))


def read_summary(query_rows, outer_state, key_total, head_count):
    count_rows = query_rows.shape[0]
    feat_query = feature_map(query_rows.astype(jnp.float32)).reshape(count_rows, head_count, -1)
    numerator = jnp.einsum("nhd,hde->nhe", feat_query, outer_state, precision=HIGHEST)
    denominator = jnp.einsum("nhd,hd->nh", feat_query, key_total, precision=HIGHEST)
    return (numerator / denominator[..., None]).reshape(count_rows, -1)


def contrast(unit_rows, peak_rows, label_part, mask_part, peak_start):
    logit_scale = 2.0 / math.sqrt(unit_rows.shape[-1])
    peak_f = peak_rows.astype(jnp.float32)
    logits = logit_scale * jnp.dot(unit_rows, peak_f.T, precision=HIGHEST)
    peak_index = peak_start + jnp.arange(peak_rows.shape[0], dtype=jnp.int32)
    target = (label_part[:, None] == peak_index[None, :]).astype(jnp.float32)
    sign_rows = 2.0 * target - 1.0
    loss_part = jnp.sum(mask_part[:, None] * jax.nn.softplus(-sign_rows * logits)) / PEAKS
    slopes = mask_part[:, None] * (jax.nn.sigmoid(logits) - target) * (1.0 / math.sqrt(PEAKS))
    unit_grad = logit_scale * jnp.dot(slopes, peak_f, precision=HIGHEST)
    return (loss_part, unit_grad)


def embed_backward(unit_rows, unit_grad, embed_scale):
    inner_mean = jnp.mean(unit_grad * unit_rows, axis=-1, keepdims=True)
    return (embed_scale * (unit_grad - unit_rows * inner_mean)).astype(jnp.bfloat16)


def shards(
    atoms_in,
    tile_ids,
    tile_vals,
    seq_lens,
    pair_labels,
    peak_embed,
    norm_gain,
    w_query,
    w_key,
    w_value,
    w_out,
    w_proj,
):
    atom_rows = atoms_in[0]
    local_rows = atom_rows.shape[0]
    gathered = message_pass(atom_rows, tile_ids[0], tile_vals[0])
    hidden_one = (atom_rows.astype(jnp.float32) + gathered.astype(jnp.float32)).astype(jnp.bfloat16)
    atom_base = lax.axis_index("atoms") * local_rows
    length_one = seq_lens[0]
    label_row = pair_labels[0]
    peak_part = peak_embed[0]
    hidden_f = hidden_one.astype(jnp.float32)
    square_sum = lax.psum(jnp.sum(hidden_f * hidden_f, axis=-1), "sec")
    row_scale = lax.rsqrt(square_sum[:, None] / D + EPSILON)
    normed = (hidden_f * row_scale * norm_gain.astype(jnp.float32)).astype(jnp.bfloat16)
    head_cols = w_query.shape[1]
    sec = lax.axis_index("sec")
    width = normed.shape[1]
    other_rows = swap_sec(normed)
    out_cols = w_out.reshape(w_out.shape[0], 2, width)
    partner = (swap_sec(peak_part), swap_sec(out_cols[:, 1 - sec, :]))

    def project(weight):
        halves = weight.reshape(2, width, weight.shape[1])
        mine = jnp.dot(normed, halves[sec], preferred_element_type=jnp.float32)
        return mine + jnp.dot(other_rows, halves[1 - sec], preferred_element_type=jnp.float32)

    query_f, key_f, value_f = tuple((project(weight) for weight in (w_query, w_key, w_value)))
    head_count = head_cols // HEAD_DIM
    atom_mask = (atom_base + jnp.arange(local_rows, dtype=jnp.int32) < length_one).astype(
        jnp.float32
    )
    outer_state, key_total = key_summary(
        key_f.astype(jnp.bfloat16), value_f.astype(jnp.bfloat16), atom_mask, head_count
    )
    state_rows = jnp.concatenate([outer_state, key_total[:, None, :]], axis=1)
    packed, partner = sum_atoms(state_rows, riders=partner)
    peak_all = join_sec(peak_part, partner[0], sec, 0)
    out_rows = join_sec(out_cols[:, sec, :], partner[1], sec, 0)
    outer_state, key_total = packed[:, :HEAD_DIM, :], packed[:, HEAD_DIM, :]
    attended = read_summary(query_f.astype(jnp.bfloat16), outer_state, key_total, head_count)
    attended_all = join_sec(attended, swap_sec(attended), sec, 1)
    out_sum = jnp.sum(attended_all * attended_all, axis=-1)
    attended_n = (attended_all * lax.rsqrt(out_sum[:, None] / (HEADS * HEAD_DIM) + EPSILON)).astype(
        jnp.bfloat16
    )
    branch = jnp.dot(attended_n, out_rows, preferred_element_type=jnp.float32)
    hidden_two = (hidden_f + branch).astype(jnp.bfloat16)
    embedded = sum_sec(jnp.dot(hidden_two, w_proj, preferred_element_type=jnp.float32))
    embed_scale = lax.rsqrt(jnp.mean(embedded * embedded, axis=-1, keepdims=True) + EPSILON)
    unit_rows = embedded * embed_scale
    loss_part, unit_grad = contrast(unit_rows, peak_all, label_row, atom_mask, 0)
    embed_grad = embed_backward(unit_rows, unit_grad, embed_scale)
    proj_part = jnp.einsum("nd,ne->de", hidden_two, embed_grad, preferred_element_type=jnp.float32)
    zero = jnp.zeros((1,), jnp.float32)
    payload = jnp.concatenate([proj_part.reshape(-1), loss_part.reshape(1), zero])
    packed = sum_atoms(payload, exact=proj_part.size)
    proj_total = packed[: proj_part.size].reshape(proj_part.shape)
    loss_sum = packed[proj_part.size] + packed[proj_part.size + 1]
    loss_total = loss_sum / (local_rows * lax.axis_size("atoms"))
    return (hidden_two[None], loss_total.reshape(1), proj_total[None])


def solution(mesh):
    return jax.shard_map(
        shards,
        mesh=mesh,
        in_specs=(
            P("batch", "atoms", "sec"),
            P("batch", None, "atoms"),
            P("batch", "atoms", None, None),
            P("batch"),
            P("batch", "atoms"),
            P("batch", "sec", None),
            P("sec"),
            P(None, "sec"),
            P(None, "sec"),
            P(None, "sec"),
            P("sec", None),
            P("sec", None),
        ),
        out_specs=(P("batch", "atoms", "sec"), P("batch"), P("batch", "sec", None)),
        check_vma=False,
    )
```

```python
import math

import jax
import jax.numpy as jnp
from jax import lax
from jax.sharding import PartitionSpec as P

D = 1024
HEADS = 8
HEAD_DIM = 64
PEAKS = 256


EPSILON = 1e-06
HIGHEST = lax.Precision.HIGHEST


def extended(x, sides, width):
    for axis, dim in sides:
        peers, length = (lax.axis_size(axis), x.shape[dim])
        up = [(i, (i + 1) % peers) for i in range(peers - 1)]
        down = [(j, i) for i, j in up]
        last = lax.slice_in_dim(x, length - width, length, axis=dim)
        leading = lax.slice_in_dim(x, 0, width, axis=dim)
        before = lax.ppermute(last, axis, up)
        after = lax.ppermute(leading, axis, down)
        x = jnp.concatenate([before, x, after], axis=dim)
    return x


def swap_sec(x):
    return lax.ppermute(x, "sec", [(0, 1), (1, 0)])


def join_sec(mine, other, sec, axis):
    first = jnp.where(sec == 0, mine, other)
    second = jnp.where(sec == 0, other, mine)
    return jnp.concatenate([first, second], axis=axis)


def sum_sec(x):
    return x + swap_sec(x)


def sum_atoms_grouped(x, riders):
    peers = lax.axis_size("atoms")
    inner = min(peers, 8)
    rows = [[g * inner + k for k in range(inner)] for g in range(peers // inner)]
    cols = [list(group) for group in zip(*rows)]
    flat = x.reshape(-1)
    lanes = -(-flat.shape[0] // 128) * 128
    flat = jnp.pad(flat, (0, lanes - flat.shape[0])).reshape(1, lanes // 128, 128)
    for groups in (rows, cols):
        copies = jnp.broadcast_to(flat, (len(groups[0]),) + flat.shape[1:])
        arrived = lax.all_to_all(copies, "atoms", 0, 0, tiled=True, axis_index_groups=groups)
        if groups is rows:
            arrived, riders = lax.optimization_barrier((arrived, riders))
        flat = jnp.sum(arrived, axis=0, keepdims=True)
    return flat.reshape(-1)[: x.size].reshape(x.shape), riders


def sum_atoms(x, exact=None, riders=None):
    peers = lax.axis_size("atoms")
    flat = x.reshape(-1)
    chunk = -(-flat.shape[0] // (peers * 128)) * 128
    flat = jnp.pad(flat, (0, chunk * peers - flat.shape[0]))
    pieces = flat.reshape(peers, chunk // 128, 128)
    arrived = lax.all_to_all(pieces, "atoms", 0, 0, tiled=True)
    if riders is not None:
        arrived, riders = lax.optimization_barrier((arrived, riders))
    owned = jnp.sum(arrived, axis=0, keepdims=True)
    if exact is not None:
        owner, slot = divmod(exact, chunk)
        rest = owned - owned.astype(jnp.bfloat16).astype(jnp.float32)
        here = lax.axis_index("atoms") == owner
        spare = (slot + 1) // 128, (slot + 1) % 128
        row = lax.broadcasted_iota(jnp.int32, owned.shape, 1)
        lane = lax.broadcasted_iota(jnp.int32, owned.shape, 2)
        target = here & (row == spare[0]) & (lane == spare[1])
        owned = jnp.where(target, rest[0, slot // 128, slot % 128], owned).astype(jnp.bfloat16)
    spread = lax.all_to_all(jnp.broadcast_to(owned, pieces.shape), "atoms", 0, 0, tiled=True)
    total = spread.reshape(-1)[: x.size].reshape(x.shape).astype(jnp.float32)
    return total if riders is None else (total, riders)


def feature_map(values):
    return jax.nn.elu(values) + 1.0


def message_pass(atom_rows, tile_pair, tile_block):
    tile_size = tile_block.shape[-1]
    local_rows, half_width = atom_rows.shape
    block_count = local_rows // tile_size
    reach_blocks = max(block_count // 2, 1)
    padded = extended(atom_rows, (("atoms", 0),), reach_blocks * tile_size)
    blocks = padded.reshape(block_count + 2 * reach_blocks, tile_size, half_width)
    first_block = lax.axis_index("atoms") * block_count
    row_ids = tile_pair[0]
    col_ids = tile_pair[1]
    live_tiles = row_ids >= 0
    col_local = jnp.where(live_tiles, col_ids - first_block + reach_blocks, 0)
    row_local = jnp.where(live_tiles, row_ids - first_block, -1)
    panels = jnp.take(blocks, col_local, axis=0)
    selector = row_local[None, :] == jnp.arange(block_count, dtype=jnp.int32)[:, None]
    masked = jnp.where(selector[:, :, None, None], tile_block[None], jnp.zeros_like(tile_block[None]))
    summed = jnp.einsum("btij,tjf->bif", masked, panels, preferred_element_type=jnp.float32)
    return summed.reshape(local_rows, half_width).astype(jnp.bfloat16)


def key_summary(key_rows, value_rows, atom_mask, head_count):
    count_rows = key_rows.shape[0]
    feat_keys = (
        feature_map(key_rows.astype(jnp.float32)).reshape(count_rows, head_count, -1)
        * atom_mask[:, None, None]
    )
    value_f = value_rows.astype(jnp.float32).reshape(count_rows, head_count, -1)
    outer_state = jnp.einsum("nhd,nhe->hde", feat_keys, value_f, precision=HIGHEST)
    return (outer_state, jnp.sum(feat_keys, axis=0))


def read_summary(query_rows, outer_state, key_total, head_count):
    count_rows = query_rows.shape[0]
    feat_query = feature_map(query_rows.astype(jnp.float32)).reshape(count_rows, head_count, -1)
    numerator = jnp.einsum("nhd,hde->nhe", feat_query, outer_state, precision=HIGHEST)
    denominator = jnp.einsum("nhd,hd->nh", feat_query, key_total, precision=HIGHEST)
    return (numerator / denominator[..., None]).reshape(count_rows, -1)


def contrast(unit_rows, peak_rows, label_part, mask_part, peak_start):
    logit_scale = 2.0 / math.sqrt(unit_rows.shape[-1])
    peak_f = peak_rows.astype(jnp.float32)
    logits = logit_scale * jnp.dot(unit_rows, peak_f.T, precision=HIGHEST)
    peak_index = peak_start + jnp.arange(peak_rows.shape[0], dtype=jnp.int32)
    target = (label_part[:, None] == peak_index[None, :]).astype(jnp.float32)
    sign_rows = 2.0 * target - 1.0
    loss_part = jnp.sum(mask_part[:, None] * jax.nn.softplus(-sign_rows * logits)) / PEAKS
    slopes = mask_part[:, None] * (jax.nn.sigmoid(logits) - target) * (1.0 / math.sqrt(PEAKS))
    unit_grad = logit_scale * jnp.dot(slopes, peak_f, precision=HIGHEST)
    return (loss_part, unit_grad)


def embed_backward(unit_rows, unit_grad, embed_scale):
    inner_mean = jnp.mean(unit_grad * unit_rows, axis=-1, keepdims=True)
    return (embed_scale * (unit_grad - unit_rows * inner_mean)).astype(jnp.bfloat16)


def shards(
    atoms_in,
    tile_ids,
    tile_vals,
    seq_lens,
    pair_labels,
    peak_embed,
    norm_gain,
    w_query,
    w_key,
    w_value,
    w_out,
    w_proj,
):
    atom_rows = atoms_in[0]
    local_rows = atom_rows.shape[0]
    gathered = message_pass(atom_rows, tile_ids[0], tile_vals[0])
    hidden_one = (atom_rows.astype(jnp.float32) + gathered.astype(jnp.float32)).astype(jnp.bfloat16)
    atom_base = lax.axis_index("atoms") * local_rows
    length_one = seq_lens[0]
    label_row = pair_labels[0]
    peak_part = peak_embed[0]
    hidden_f = hidden_one.astype(jnp.float32)
    square_sum = lax.psum(jnp.sum(hidden_f * hidden_f, axis=-1), "sec")
    row_scale = lax.rsqrt(square_sum[:, None] / D + EPSILON)
    normed = (hidden_f * row_scale * norm_gain.astype(jnp.float32)).astype(jnp.bfloat16)
    head_cols = w_query.shape[1]
    sec = lax.axis_index("sec")
    width = normed.shape[1]
    other_rows = swap_sec(normed)
    out_cols = w_out.reshape(w_out.shape[0], 2, width)
    partner = (swap_sec(peak_part), swap_sec(out_cols[:, 1 - sec, :]))

    def project(weight):
        halves = weight.reshape(2, width, weight.shape[1])
        mine = jnp.dot(normed, halves[sec], preferred_element_type=jnp.float32)
        return mine + jnp.dot(other_rows, halves[1 - sec], preferred_element_type=jnp.float32)

    query_f, key_f, value_f = tuple((project(weight) for weight in (w_query, w_key, w_value)))
    head_count = head_cols // HEAD_DIM
    atom_mask = (atom_base + jnp.arange(local_rows, dtype=jnp.int32) < length_one).astype(
        jnp.float32
    )
    outer_state, key_total = key_summary(
        key_f.astype(jnp.bfloat16), value_f.astype(jnp.bfloat16), atom_mask, head_count
    )
    state_rows = jnp.concatenate([outer_state, key_total[:, None, :]], axis=1)
    packed, partner = sum_atoms_grouped(state_rows, partner)
    peak_all = join_sec(peak_part, partner[0], sec, 0)
    out_rows = join_sec(out_cols[:, sec, :], partner[1], sec, 0)
    outer_state, key_total = packed[:, :HEAD_DIM, :], packed[:, HEAD_DIM, :]
    attended = read_summary(query_f.astype(jnp.bfloat16), outer_state, key_total, head_count)
    attended_all = join_sec(attended, swap_sec(attended), sec, 1)
    out_sum = jnp.sum(attended_all * attended_all, axis=-1)
    attended_n = (attended_all * lax.rsqrt(out_sum[:, None] / (HEADS * HEAD_DIM) + EPSILON)).astype(
        jnp.bfloat16
    )
    branch = jnp.dot(attended_n, out_rows, preferred_element_type=jnp.float32)
    hidden_two = (hidden_f + branch).astype(jnp.bfloat16)
    embedded = sum_sec(jnp.dot(hidden_two, w_proj, preferred_element_type=jnp.float32))
    embed_scale = lax.rsqrt(jnp.mean(embedded * embedded, axis=-1, keepdims=True) + EPSILON)
    unit_rows = embedded * embed_scale
    loss_part, unit_grad = contrast(unit_rows, peak_all, label_row, atom_mask, 0)
    embed_grad = embed_backward(unit_rows, unit_grad, embed_scale)
    proj_part = jnp.einsum("nd,ne->de", hidden_two, embed_grad, preferred_element_type=jnp.float32)
    zero = jnp.zeros((1,), jnp.float32)
    payload = jnp.concatenate([proj_part.reshape(-1), loss_part.reshape(1), zero])
    packed = sum_atoms(payload, exact=proj_part.size)
    proj_total = packed[: proj_part.size].reshape(proj_part.shape)
    loss_sum = packed[proj_part.size] + packed[proj_part.size + 1]
    loss_total = loss_sum / (local_rows * lax.axis_size("atoms"))
    return (hidden_two[None], loss_total.reshape(1), proj_total[None])


def solution(mesh):
    return jax.shard_map(
        shards,
        mesh=mesh,
        in_specs=(
            P("batch", "atoms", "sec"),
            P("batch", None, "atoms"),
            P("batch", "atoms", None, None),
            P("batch"),
            P("batch", "atoms"),
            P("batch", "sec", None),
            P("sec"),
            P(None, "sec"),
            P(None, "sec"),
            P(None, "sec"),
            P("sec", None),
            P("sec", None),
        ),
        out_specs=(P("batch", "atoms", "sec"), P("batch"), P("batch", "sec", None)),
        check_vma=False,
    )
```

```python
import math

import jax
import jax.numpy as jnp
from jax import lax
from jax.sharding import PartitionSpec as P

D = 1024
HEADS = 8
HEAD_DIM = 64
PEAKS = 256


EPSILON = 1e-06
PRECISION = lax.Precision.HIGH


def extended(x, sides, width):
    for axis, dim in sides:
        peers, length = (lax.axis_size(axis), x.shape[dim])
        up = [(i, (i + 1) % peers) for i in range(peers - 1)]
        down = [(j, i) for i, j in up]
        last = lax.slice_in_dim(x, length - width, length, axis=dim)
        leading = lax.slice_in_dim(x, 0, width, axis=dim)
        before = lax.ppermute(last, axis, up)
        after = lax.ppermute(leading, axis, down)
        x = jnp.concatenate([before, x, after], axis=dim)
    return x


def swap_sec(x):
    return lax.ppermute(x, "sec", [(0, 1), (1, 0)])


def join_sec(mine, other, sec, axis):
    first = jnp.where(sec == 0, mine, other)
    second = jnp.where(sec == 0, other, mine)
    return jnp.concatenate([first, second], axis=axis)


def sum_sec(x):
    return x + swap_sec(x)


def sum_atoms(x, exact=None, riders=None):
    peers = lax.axis_size("atoms")
    flat = x.reshape(-1)
    chunk = -(-flat.shape[0] // (peers * 128)) * 128
    flat = jnp.pad(flat, (0, chunk * peers - flat.shape[0]))
    pieces = flat.reshape(peers, chunk // 128, 128)
    arrived = lax.all_to_all(pieces, "atoms", 0, 0, tiled=True)
    if riders is not None:
        arrived, riders = lax.optimization_barrier((arrived, riders))
    owned = jnp.sum(arrived, axis=0, keepdims=True)
    if exact is not None:
        owner, slot = divmod(exact, chunk)
        rest = owned - owned.astype(jnp.bfloat16).astype(jnp.float32)
        here = lax.axis_index("atoms") == owner
        spare = (slot + 1) // 128, (slot + 1) % 128
        row = lax.broadcasted_iota(jnp.int32, owned.shape, 1)
        lane = lax.broadcasted_iota(jnp.int32, owned.shape, 2)
        target = here & (row == spare[0]) & (lane == spare[1])
        owned = jnp.where(target, rest[0, slot // 128, slot % 128], owned).astype(jnp.bfloat16)
    spread = lax.all_to_all(jnp.broadcast_to(owned, pieces.shape), "atoms", 0, 0, tiled=True)
    total = spread.reshape(-1)[: x.size].reshape(x.shape).astype(jnp.float32)
    return total if riders is None else (total, riders)


def feature_map(values):
    return jax.nn.elu(values) + 1.0


def message_pass(atom_rows, tile_pair, tile_block):
    tile_size = tile_block.shape[-1]
    local_rows, half_width = atom_rows.shape
    block_count = local_rows // tile_size
    reach_blocks = max(block_count // 2, 1)
    padded = extended(atom_rows, (("atoms", 0),), reach_blocks * tile_size)
    blocks = padded.reshape(block_count + 2 * reach_blocks, tile_size, half_width)
    first_block = lax.axis_index("atoms") * block_count
    row_ids = tile_pair[0]
    col_ids = tile_pair[1]
    live_tiles = row_ids >= 0
    col_local = jnp.where(live_tiles, col_ids - first_block + reach_blocks, 0)
    row_local = jnp.where(live_tiles, row_ids - first_block, -1)
    panels = jnp.take(blocks, col_local, axis=0)
    selector = row_local[None, :] == jnp.arange(block_count, dtype=jnp.int32)[:, None]
    masked = jnp.where(selector[:, :, None, None], tile_block[None], jnp.zeros_like(tile_block[None]))
    summed = jnp.einsum("btij,tjf->bif", masked, panels, preferred_element_type=jnp.float32)
    return summed.reshape(local_rows, half_width).astype(jnp.bfloat16)


def key_summary(key_rows, value_rows, atom_mask, head_count):
    count_rows = key_rows.shape[0]
    feat_keys = (
        feature_map(key_rows.astype(jnp.float32)).reshape(count_rows, head_count, -1)
        * atom_mask[:, None, None]
    )
    value_f = value_rows.astype(jnp.float32).reshape(count_rows, head_count, -1)
    outer_state = jnp.einsum("nhd,nhe->hde", feat_keys, value_f, precision=PRECISION)
    return (outer_state, jnp.sum(feat_keys, axis=0))


def read_summary(query_rows, outer_state, key_total, head_count):
    count_rows = query_rows.shape[0]
    feat_query = feature_map(query_rows.astype(jnp.float32)).reshape(count_rows, head_count, -1)
    numerator = jnp.einsum("nhd,hde->nhe", feat_query, outer_state, precision=PRECISION)
    denominator = jnp.einsum("nhd,hd->nh", feat_query, key_total, precision=PRECISION)
    return (numerator / denominator[..., None]).reshape(count_rows, -1)


def contrast(unit_rows, peak_rows, label_part, mask_part, peak_start):
    logit_scale = 2.0 / math.sqrt(unit_rows.shape[-1])
    peak_f = peak_rows.astype(jnp.float32)
    logits = logit_scale * jnp.dot(unit_rows, peak_f.T, precision=PRECISION)
    peak_index = peak_start + jnp.arange(peak_rows.shape[0], dtype=jnp.int32)
    target = (label_part[:, None] == peak_index[None, :]).astype(jnp.float32)
    sign_rows = 2.0 * target - 1.0
    loss_part = jnp.sum(mask_part[:, None] * jax.nn.softplus(-sign_rows * logits)) / PEAKS
    slopes = mask_part[:, None] * (jax.nn.sigmoid(logits) - target) * (1.0 / math.sqrt(PEAKS))
    unit_grad = logit_scale * jnp.dot(slopes, peak_f, precision=PRECISION)
    return (loss_part, unit_grad)


def embed_backward(unit_rows, unit_grad, embed_scale):
    inner_mean = jnp.mean(unit_grad * unit_rows, axis=-1, keepdims=True)
    return (embed_scale * (unit_grad - unit_rows * inner_mean)).astype(jnp.bfloat16)


def shards(
    atoms_in,
    tile_ids,
    tile_vals,
    seq_lens,
    pair_labels,
    peak_embed,
    norm_gain,
    w_query,
    w_key,
    w_value,
    w_out,
    w_proj,
):
    atom_rows = atoms_in[0]
    local_rows = atom_rows.shape[0]
    gathered = message_pass(atom_rows, tile_ids[0], tile_vals[0])
    hidden_one = (atom_rows.astype(jnp.float32) + gathered.astype(jnp.float32)).astype(jnp.bfloat16)
    atom_base = lax.axis_index("atoms") * local_rows
    length_one = seq_lens[0]
    label_row = pair_labels[0]
    peak_part = peak_embed[0]
    hidden_f = hidden_one.astype(jnp.float32)
    square_sum = lax.psum(jnp.sum(hidden_f * hidden_f, axis=-1), "sec")
    row_scale = lax.rsqrt(square_sum[:, None] / D + EPSILON)
    normed = (hidden_f * row_scale * norm_gain.astype(jnp.float32)).astype(jnp.bfloat16)
    head_cols = w_query.shape[1]
    sec = lax.axis_index("sec")
    width = normed.shape[1]
    other_rows = swap_sec(normed)
    out_cols = w_out.reshape(w_out.shape[0], 2, width)
    partner = (swap_sec(peak_part), swap_sec(out_cols[:, 1 - sec, :]))

    def project(weight):
        halves = weight.reshape(2, width, weight.shape[1])
        mine = jnp.dot(normed, halves[sec], preferred_element_type=jnp.float32)
        return mine + jnp.dot(other_rows, halves[1 - sec], preferred_element_type=jnp.float32)

    query_f, key_f, value_f = tuple((project(weight) for weight in (w_query, w_key, w_value)))
    head_count = head_cols // HEAD_DIM
    atom_mask = (atom_base + jnp.arange(local_rows, dtype=jnp.int32) < length_one).astype(
        jnp.float32
    )
    outer_state, key_total = key_summary(
        key_f.astype(jnp.bfloat16), value_f.astype(jnp.bfloat16), atom_mask, head_count
    )
    state_rows = jnp.concatenate([outer_state, key_total[:, None, :]], axis=1)
    packed, partner = sum_atoms(state_rows, riders=partner)
    peak_all = join_sec(peak_part, partner[0], sec, 0)
    out_rows = join_sec(out_cols[:, sec, :], partner[1], sec, 0)
    outer_state, key_total = packed[:, :HEAD_DIM, :], packed[:, HEAD_DIM, :]
    attended = read_summary(query_f.astype(jnp.bfloat16), outer_state, key_total, head_count)
    attended_all = join_sec(attended, swap_sec(attended), sec, 1)
    out_sum = jnp.sum(attended_all * attended_all, axis=-1)
    attended_n = (attended_all * lax.rsqrt(out_sum[:, None] / (HEADS * HEAD_DIM) + EPSILON)).astype(
        jnp.bfloat16
    )
    branch = jnp.dot(attended_n, out_rows, preferred_element_type=jnp.float32)
    hidden_two = (hidden_f + branch).astype(jnp.bfloat16)
    embedded = sum_sec(jnp.dot(hidden_two, w_proj, preferred_element_type=jnp.float32))
    embed_scale = lax.rsqrt(jnp.mean(embedded * embedded, axis=-1, keepdims=True) + EPSILON)
    unit_rows = embedded * embed_scale
    loss_part, unit_grad = contrast(unit_rows, peak_all, label_row, atom_mask, 0)
    embed_grad = embed_backward(unit_rows, unit_grad, embed_scale)
    proj_part = jnp.einsum("nd,ne->de", hidden_two, embed_grad, preferred_element_type=jnp.float32)
    zero = jnp.zeros((1,), jnp.float32)
    payload = jnp.concatenate([proj_part.reshape(-1), loss_part.reshape(1), zero])
    packed = sum_atoms(payload, exact=proj_part.size)
    proj_total = packed[: proj_part.size].reshape(proj_part.shape)
    loss_sum = packed[proj_part.size] + packed[proj_part.size + 1]
    loss_total = loss_sum / (local_rows * lax.axis_size("atoms"))
    return (hidden_two[None], loss_total.reshape(1), proj_total[None])


def solution(mesh):
    return jax.shard_map(
        shards,
        mesh=mesh,
        in_specs=(
            P("batch", "atoms", "sec"),
            P("batch", None, "atoms"),
            P("batch", "atoms", None, None),
            P("batch"),
            P("batch", "atoms"),
            P("batch", "sec", None),
            P("sec"),
            P(None, "sec"),
            P(None, "sec"),
            P(None, "sec"),
            P("sec", None),
            P("sec", None),
        ),
        out_specs=(P("batch", "atoms", "sec"), P("batch"), P("batch", "sec", None)),
        check_vma=False,
    )
```

```python
import math

import jax
import jax.numpy as jnp
from jax import lax
from jax.sharding import PartitionSpec as P

D = 1024
HEADS = 8
HEAD_DIM = 64
PEAKS = 256


EPSILON = 1e-06
HIGHEST = lax.Precision.HIGHEST


def extended(x, sides, width):
    for axis, dim in sides:
        peers, length = (lax.axis_size(axis), x.shape[dim])
        up = [(i, (i + 1) % peers) for i in range(peers - 1)]
        down = [(j, i) for i, j in up]
        last = lax.slice_in_dim(x, length - width, length, axis=dim)
        leading = lax.slice_in_dim(x, 0, width, axis=dim)
        before = lax.ppermute(last, axis, up)
        after = lax.ppermute(leading, axis, down)
        x = jnp.concatenate([before, x, after], axis=dim)
    return x


def swap_sec(x):
    return lax.ppermute(x, "sec", [(0, 1), (1, 0)])


def join_sec(mine, other, sec, axis):
    first = jnp.where(sec == 0, mine, other)
    second = jnp.where(sec == 0, other, mine)
    return jnp.concatenate([first, second], axis=axis)


def sum_sec(x):
    return x + swap_sec(x)


def sum_atoms(x, exact=None, riders=None):
    peers = lax.axis_size("atoms")
    flat = x.reshape(-1)
    chunk = -(-flat.shape[0] // (peers * 128)) * 128
    flat = jnp.pad(flat, (0, chunk * peers - flat.shape[0]))
    pieces = flat.reshape(peers, chunk // 128, 128)
    arrived = lax.all_to_all(pieces, "atoms", 0, 0, tiled=True)
    if riders is not None:
        arrived, riders = lax.optimization_barrier((arrived, riders))
    owned = jnp.sum(arrived, axis=0, keepdims=True)
    if exact is not None:
        owner, slot = divmod(exact, chunk)
        rest = owned - owned.astype(jnp.bfloat16).astype(jnp.float32)
        here = lax.axis_index("atoms") == owner
        spare = (slot + 1) // 128, (slot + 1) % 128
        row = lax.broadcasted_iota(jnp.int32, owned.shape, 1)
        lane = lax.broadcasted_iota(jnp.int32, owned.shape, 2)
        target = here & (row == spare[0]) & (lane == spare[1])
        owned = jnp.where(target, rest[0, slot // 128, slot % 128], owned).astype(jnp.bfloat16)
    spread = lax.all_to_all(jnp.broadcast_to(owned, pieces.shape), "atoms", 0, 0, tiled=True)
    total = spread.reshape(-1)[: x.size].reshape(x.shape).astype(jnp.float32)
    return total if riders is None else (total, riders)


def feature_map(values):
    return jax.nn.elu(values) + 1.0


def message_pass(atom_rows, tile_pair, tile_block):
    tile_size = tile_block.shape[-1]
    local_rows, half_width = atom_rows.shape
    block_count = local_rows // tile_size
    reach_blocks = max(block_count // 2, 1)
    padded = extended(atom_rows, (("atoms", 0),), reach_blocks * tile_size)
    blocks = padded.reshape(block_count + 2 * reach_blocks, tile_size, half_width)
    first_block = lax.axis_index("atoms") * block_count
    row_ids = tile_pair[0]
    col_ids = tile_pair[1]
    live_tiles = row_ids >= 0
    col_local = jnp.where(live_tiles, col_ids - first_block + reach_blocks, 0)
    row_local = jnp.where(live_tiles, row_ids - first_block, -1)
    panels = jnp.take(blocks, col_local, axis=0)
    selector = row_local[None, :] == jnp.arange(block_count, dtype=jnp.int32)[:, None]
    masked = jnp.where(selector[:, :, None, None], tile_block[None], jnp.zeros_like(tile_block[None]))
    summed = jnp.einsum("btij,tjf->bif", masked, panels, preferred_element_type=jnp.float32)
    return summed.reshape(local_rows, half_width).astype(jnp.bfloat16)


def key_summary(key_rows, value_rows, atom_mask, head_count):
    count_rows = key_rows.shape[0]
    feat_keys = (
        feature_map(key_rows.astype(jnp.float32)).reshape(count_rows, head_count, -1)
        * atom_mask[:, None, None]
    )
    value_f = value_rows.astype(jnp.float32).reshape(count_rows, head_count, -1)
    outer_state = jnp.einsum("nhd,nhe->hde", feat_keys, value_f, precision=HIGHEST)
    return (outer_state, jnp.sum(feat_keys, axis=0))


def read_summary(query_rows, outer_state, key_total, head_count):
    count_rows = query_rows.shape[0]
    feat_query = feature_map(query_rows.astype(jnp.float32)).reshape(count_rows, head_count, -1)
    numerator = jnp.einsum("nhd,hde->nhe", feat_query, outer_state, precision=HIGHEST)
    denominator = jnp.einsum("nhd,hd->nh", feat_query, key_total, precision=HIGHEST)
    return (numerator / denominator[..., None]).reshape(count_rows, -1)


def contrast(unit_rows, peak_rows, label_part, mask_part, peak_start):
    logit_scale = 2.0 / math.sqrt(unit_rows.shape[-1])
    peak_f = peak_rows.astype(jnp.float32)
    logits = logit_scale * jnp.dot(unit_rows, peak_f.T, precision=HIGHEST)
    peak_index = peak_start + jnp.arange(peak_rows.shape[0], dtype=jnp.int32)
    target = (label_part[:, None] == peak_index[None, :]).astype(jnp.float32)
    sign_rows = 2.0 * target - 1.0
    loss_part = jnp.sum(mask_part[:, None] * jax.nn.softplus(-sign_rows * logits)) / PEAKS
    slopes = mask_part[:, None] * (jax.nn.sigmoid(logits) - target) * (1.0 / math.sqrt(PEAKS))
    unit_grad = logit_scale * jnp.dot(slopes, peak_f, precision=HIGHEST)
    return (loss_part, unit_grad)


def embed_backward(unit_rows, unit_grad, embed_scale):
    inner_mean = jnp.mean(unit_grad * unit_rows, axis=-1, keepdims=True)
    return (embed_scale * (unit_grad - unit_rows * inner_mean)).astype(jnp.bfloat16)


def shards(
    atoms_in,
    tile_ids,
    tile_vals,
    seq_lens,
    pair_labels,
    peak_embed,
    norm_gain,
    w_query,
    w_key,
    w_value,
    w_out,
    w_proj,
):
    atom_rows = atoms_in[0]
    local_rows = atom_rows.shape[0]
    gathered = message_pass(atom_rows, tile_ids[0], tile_vals[0])
    hidden_one = (atom_rows.astype(jnp.float32) + gathered.astype(jnp.float32)).astype(jnp.bfloat16)
    atom_base = lax.axis_index("atoms") * local_rows
    length_one = seq_lens[0]
    label_row = pair_labels[0]
    peak_part = peak_embed[0]
    hidden_f = hidden_one.astype(jnp.float32)
    square_part = jnp.sum(hidden_f * hidden_f, axis=-1)
    square_sum = square_part + swap_sec(square_part)
    row_scale = lax.rsqrt(square_sum[:, None] / D + EPSILON)
    normed = (hidden_f * row_scale * norm_gain.astype(jnp.float32)).astype(jnp.bfloat16)
    head_cols = w_query.shape[1]
    sec = lax.axis_index("sec")
    width = normed.shape[1]
    other_rows = swap_sec(normed)
    out_cols = w_out.reshape(w_out.shape[0], 2, width)
    partner = (swap_sec(peak_part), swap_sec(out_cols[:, 1 - sec, :]))

    def project(weight):
        halves = weight.reshape(2, width, weight.shape[1])
        mine = jnp.dot(normed, halves[sec], preferred_element_type=jnp.float32)
        return mine + jnp.dot(other_rows, halves[1 - sec], preferred_element_type=jnp.float32)

    query_f, key_f, value_f = tuple((project(weight) for weight in (w_query, w_key, w_value)))
    head_count = head_cols // HEAD_DIM
    atom_mask = (atom_base + jnp.arange(local_rows, dtype=jnp.int32) < length_one).astype(
        jnp.float32
    )
    outer_state, key_total = key_summary(
        key_f.astype(jnp.bfloat16), value_f.astype(jnp.bfloat16), atom_mask, head_count
    )
    state_rows = jnp.concatenate([outer_state, key_total[:, None, :]], axis=1)
    packed, partner = sum_atoms(state_rows, riders=partner)
    peak_all = join_sec(peak_part, partner[0], sec, 0)
    out_rows = join_sec(out_cols[:, sec, :], partner[1], sec, 0)
    outer_state, key_total = packed[:, :HEAD_DIM, :], packed[:, HEAD_DIM, :]
    attended = read_summary(query_f.astype(jnp.bfloat16), outer_state, key_total, head_count)
    attended_all = join_sec(attended, swap_sec(attended), sec, 1)
    out_sum = jnp.sum(attended_all * attended_all, axis=-1)
    attended_n = (attended_all * lax.rsqrt(out_sum[:, None] / (HEADS * HEAD_DIM) + EPSILON)).astype(
        jnp.bfloat16
    )
    branch = jnp.dot(attended_n, out_rows, preferred_element_type=jnp.float32)
    hidden_two = (hidden_f + branch).astype(jnp.bfloat16)
    embedded = sum_sec(jnp.dot(hidden_two, w_proj, preferred_element_type=jnp.float32))
    embed_scale = lax.rsqrt(jnp.mean(embedded * embedded, axis=-1, keepdims=True) + EPSILON)
    unit_rows = embedded * embed_scale
    loss_part, unit_grad = contrast(unit_rows, peak_all, label_row, atom_mask, 0)
    embed_grad = embed_backward(unit_rows, unit_grad, embed_scale)
    proj_part = jnp.einsum("nd,ne->de", hidden_two, embed_grad, preferred_element_type=jnp.float32)
    zero = jnp.zeros((1,), jnp.float32)
    payload = jnp.concatenate([proj_part.reshape(-1), loss_part.reshape(1), zero])
    packed = sum_atoms(payload, exact=proj_part.size)
    proj_total = packed[: proj_part.size].reshape(proj_part.shape)
    loss_sum = packed[proj_part.size] + packed[proj_part.size + 1]
    loss_total = loss_sum / (local_rows * lax.axis_size("atoms"))
    return (hidden_two[None], loss_total.reshape(1), proj_total[None])


def solution(mesh):
    return jax.shard_map(
        shards,
        mesh=mesh,
        in_specs=(
            P("batch", "atoms", "sec"),
            P("batch", None, "atoms"),
            P("batch", "atoms", None, None),
            P("batch"),
            P("batch", "atoms"),
            P("batch", "sec", None),
            P("sec"),
            P(None, "sec"),
            P(None, "sec"),
            P(None, "sec"),
            P("sec", None),
            P("sec", None),
        ),
        out_specs=(P("batch", "atoms", "sec"), P("batch"), P("batch", "sec", None)),
        check_vma=False,
    )
```

```python
import math

import jax
import jax.numpy as jnp
from jax import lax
from jax.sharding import PartitionSpec as P

D = 1024
HEADS = 8
HEAD_DIM = 64
PEAKS = 256


EPSILON = 1e-06
HIGHEST = lax.Precision.HIGHEST


def extended(x, sides, width):
    for axis, dim in sides:
        peers, length = (lax.axis_size(axis), x.shape[dim])
        up = [(i, (i + 1) % peers) for i in range(peers - 1)]
        down = [(j, i) for i, j in up]
        last = lax.slice_in_dim(x, length - width, length, axis=dim)
        leading = lax.slice_in_dim(x, 0, width, axis=dim)
        before = lax.ppermute(last, axis, up)
        after = lax.ppermute(leading, axis, down)
        x = jnp.concatenate([before, x, after], axis=dim)
    return x


def swap_sec(x):
    return lax.ppermute(x, "sec", [(0, 1), (1, 0)])


def join_sec(mine, other, sec, axis):
    first = jnp.where(sec == 0, mine, other)
    second = jnp.where(sec == 0, other, mine)
    return jnp.concatenate([first, second], axis=axis)


def sum_sec(x):
    return x + swap_sec(x)


def sum_atoms(x, exact=None, riders=None):
    peers = lax.axis_size("atoms")
    flat = x.reshape(-1)
    chunk = -(-flat.shape[0] // (peers * 128)) * 128
    flat = jnp.pad(flat, (0, chunk * peers - flat.shape[0]))
    pieces = flat.reshape(peers, chunk // 128, 128)
    arrived = lax.all_to_all(pieces, "atoms", 0, 0, tiled=True)
    if riders is not None:
        arrived, riders = lax.optimization_barrier((arrived, riders))
    owned = jnp.sum(arrived, axis=0, keepdims=True)
    if exact is not None:
        owner, slot = divmod(exact, chunk)
        rest = owned - owned.astype(jnp.bfloat16).astype(jnp.float32)
        here = lax.axis_index("atoms") == owner
        spare = (slot + 1) // 128, (slot + 1) % 128
        row = lax.broadcasted_iota(jnp.int32, owned.shape, 1)
        lane = lax.broadcasted_iota(jnp.int32, owned.shape, 2)
        target = here & (row == spare[0]) & (lane == spare[1])
        owned = jnp.where(target, rest[0, slot // 128, slot % 128], owned).astype(jnp.bfloat16)
    spread = lax.all_to_all(jnp.broadcast_to(owned, pieces.shape), "atoms", 0, 0, tiled=True)
    total = spread.reshape(-1)[: x.size].reshape(x.shape)
    return total if riders is None else (total, riders)


def feature_map(values):
    return jax.nn.elu(values) + 1.0


def message_pass(atom_rows, tile_pair, tile_block):
    tile_size = tile_block.shape[-1]
    local_rows, half_width = atom_rows.shape
    block_count = local_rows // tile_size
    reach_blocks = max(block_count // 2, 1)
    padded = extended(atom_rows, (("atoms", 0),), reach_blocks * tile_size)
    blocks = padded.reshape(block_count + 2 * reach_blocks, tile_size, half_width)
    first_block = lax.axis_index("atoms") * block_count
    row_ids = tile_pair[0]
    col_ids = tile_pair[1]
    live_tiles = row_ids >= 0
    col_local = jnp.where(live_tiles, col_ids - first_block + reach_blocks, 0)
    row_local = jnp.where(live_tiles, row_ids - first_block, -1)
    panels = jnp.take(blocks, col_local, axis=0)
    selector = row_local[None, :] == jnp.arange(block_count, dtype=jnp.int32)[:, None]
    masked = jnp.where(selector[:, :, None, None], tile_block[None], jnp.zeros_like(tile_block[None]))
    summed = jnp.einsum("btij,tjf->bif", masked, panels, preferred_element_type=jnp.float32)
    return summed.reshape(local_rows, half_width).astype(jnp.bfloat16)


def key_summary(key_rows, value_rows, atom_mask, head_count):
    count_rows = key_rows.shape[0]
    feat_keys = (
        feature_map(key_rows.astype(jnp.float32)).reshape(count_rows, head_count, -1)
        * atom_mask[:, None, None]
    )
    value_f = value_rows.astype(jnp.float32).reshape(count_rows, head_count, -1)
    outer_state = jnp.einsum("nhd,nhe->hde", feat_keys, value_f, precision=HIGHEST)
    return (outer_state, jnp.sum(feat_keys, axis=0))


def read_summary(query_rows, outer_state, key_total, head_count):
    count_rows = query_rows.shape[0]
    feat_query = feature_map(query_rows.astype(jnp.float32)).reshape(count_rows, head_count, -1)
    numerator = jnp.einsum("nhd,hde->nhe", feat_query, outer_state, precision=HIGHEST)
    denominator = jnp.einsum("nhd,hd->nh", feat_query, key_total, precision=HIGHEST)
    return (numerator / denominator[..., None]).reshape(count_rows, -1)


def contrast(unit_rows, peak_rows, label_part, mask_part, peak_start):
    logit_scale = 2.0 / math.sqrt(unit_rows.shape[-1])
    peak_f = peak_rows.astype(jnp.float32)
    logits = logit_scale * jnp.dot(unit_rows, peak_f.T, precision=HIGHEST)
    peak_index = peak_start + jnp.arange(peak_rows.shape[0], dtype=jnp.int32)
    target = (label_part[:, None] == peak_index[None, :]).astype(jnp.float32)
    sign_rows = 2.0 * target - 1.0
    loss_part = jnp.sum(mask_part[:, None] * jax.nn.softplus(-sign_rows * logits)) / PEAKS
    slopes = mask_part[:, None] * (jax.nn.sigmoid(logits) - target) * (1.0 / math.sqrt(PEAKS))
    unit_grad = logit_scale * jnp.dot(slopes, peak_f, precision=HIGHEST)
    return (loss_part, unit_grad)


def embed_backward(unit_rows, unit_grad, embed_scale):
    inner_mean = jnp.mean(unit_grad * unit_rows, axis=-1, keepdims=True)
    return (embed_scale * (unit_grad - unit_rows * inner_mean)).astype(jnp.bfloat16)


def shards(
    atoms_in,
    tile_ids,
    tile_vals,
    seq_lens,
    pair_labels,
    peak_embed,
    norm_gain,
    w_query,
    w_key,
    w_value,
    w_out,
    w_proj,
):
    atom_rows = atoms_in[0]
    local_rows = atom_rows.shape[0]
    gathered = message_pass(atom_rows, tile_ids[0], tile_vals[0])
    hidden_one = (atom_rows.astype(jnp.float32) + gathered.astype(jnp.float32)).astype(jnp.bfloat16)
    atom_base = lax.axis_index("atoms") * local_rows
    length_one = seq_lens[0]
    label_row = pair_labels[0]
    peak_part = peak_embed[0]
    hidden_f = hidden_one.astype(jnp.float32)
    square_part = jnp.sum(hidden_f * hidden_f, axis=-1)
    square_sum = square_part + swap_sec(square_part)
    row_scale = lax.rsqrt(square_sum[:, None] / D + EPSILON)
    normed = (hidden_f * row_scale * norm_gain.astype(jnp.float32)).astype(jnp.bfloat16)
    head_cols = w_query.shape[1]
    sec = lax.axis_index("sec")
    width = normed.shape[1]
    other_rows = swap_sec(normed)
    out_cols = w_out.reshape(w_out.shape[0], 2, width)
    partner = (swap_sec(peak_part), swap_sec(out_cols[:, 1 - sec, :]))

    def project(weight):
        halves = weight.reshape(2, width, weight.shape[1])
        mine = jnp.dot(normed, halves[sec], preferred_element_type=jnp.float32)
        return mine + jnp.dot(other_rows, halves[1 - sec], preferred_element_type=jnp.float32)

    query_f, key_f, value_f = tuple((project(weight) for weight in (w_query, w_key, w_value)))
    head_count = head_cols // HEAD_DIM
    atom_mask = (atom_base + jnp.arange(local_rows, dtype=jnp.int32) < length_one).astype(
        jnp.float32
    )
    outer_state, key_total = key_summary(
        key_f.astype(jnp.bfloat16), value_f.astype(jnp.bfloat16), atom_mask, head_count
    )
    state_rows = jnp.concatenate([outer_state, key_total[:, None, :]], axis=1)
    packed, partner = sum_atoms(state_rows, riders=partner)
    peak_all = join_sec(peak_part, partner[0], sec, 0)
    out_rows = join_sec(out_cols[:, sec, :], partner[1], sec, 0)
    outer_state, key_total = packed[:, :HEAD_DIM, :], packed[:, HEAD_DIM, :]
    attended = read_summary(query_f.astype(jnp.bfloat16), outer_state, key_total, head_count)
    attended_all = join_sec(attended, swap_sec(attended), sec, 1)
    out_sum = jnp.sum(attended_all * attended_all, axis=-1)
    attended_n = (attended_all * lax.rsqrt(out_sum[:, None] / (HEADS * HEAD_DIM) + EPSILON)).astype(
        jnp.bfloat16
    )
    branch = jnp.dot(attended_n, out_rows, preferred_element_type=jnp.float32)
    hidden_two = (hidden_f + branch).astype(jnp.bfloat16)
    embedded = sum_sec(jnp.dot(hidden_two, w_proj, preferred_element_type=jnp.float32))
    embed_scale = lax.rsqrt(jnp.mean(embedded * embedded, axis=-1, keepdims=True) + EPSILON)
    unit_rows = embedded * embed_scale
    loss_part, unit_grad = contrast(unit_rows, peak_all, label_row, atom_mask, 0)
    embed_grad = embed_backward(unit_rows, unit_grad, embed_scale)
    proj_part = jnp.einsum("nd,ne->de", hidden_two, embed_grad, preferred_element_type=jnp.float32)
    zero = jnp.zeros((1,), jnp.float32)
    payload = jnp.concatenate([proj_part.reshape(-1), loss_part.reshape(1), zero])
    packed = sum_atoms(payload, exact=proj_part.size)
    proj_total = packed[: proj_part.size].reshape(proj_part.shape).astype(jnp.float32)
    loss_sum = packed[proj_part.size].astype(jnp.float32) + packed[proj_part.size + 1].astype(
        jnp.float32
    )
    loss_total = loss_sum / (local_rows * lax.axis_size("atoms"))
    return (hidden_two[None], loss_total.reshape(1), proj_total[None])


def solution(mesh):
    return jax.shard_map(
        shards,
        mesh=mesh,
        in_specs=(
            P("batch", "atoms", "sec"),
            P("batch", None, "atoms"),
            P("batch", "atoms", None, None),
            P("batch"),
            P("batch", "atoms"),
            P("batch", "sec", None),
            P("sec"),
            P(None, "sec"),
            P(None, "sec"),
            P(None, "sec"),
            P("sec", None),
            P("sec", None),
        ),
        out_specs=(P("batch", "atoms", "sec"), P("batch"), P("batch", "sec", None)),
        check_vma=False,
    )
```

```python
import math

import jax
import jax.numpy as jnp
from jax import lax
from jax.sharding import PartitionSpec as P

D = 1024
HEADS = 8
HEAD_DIM = 64
PEAKS = 256


EPSILON = 1e-06
HIGHEST = lax.Precision.HIGHEST


def extended(x, sides, width):
    for axis, dim in sides:
        peers, length = (lax.axis_size(axis), x.shape[dim])
        up = [(i, (i + 1) % peers) for i in range(peers - 1)]
        down = [(j, i) for i, j in up]
        last = lax.slice_in_dim(x, length - width, length, axis=dim)
        leading = lax.slice_in_dim(x, 0, width, axis=dim)
        before = lax.ppermute(last, axis, up)
        after = lax.ppermute(leading, axis, down)
        x = jnp.concatenate([before, x, after], axis=dim)
    return x


def swap_sec(x):
    return lax.ppermute(x, "sec", [(0, 1), (1, 0)])


def join_sec(mine, other, sec, axis):
    first = jnp.where(sec == 0, mine, other)
    second = jnp.where(sec == 0, other, mine)
    return jnp.concatenate([first, second], axis=axis)


def sum_sec(x):
    return x + swap_sec(x)


def sum_atoms(x, exact=None, riders=None):
    peers = lax.axis_size("atoms")
    flat = x.reshape(-1)
    chunk = -(-flat.shape[0] // (peers * 128)) * 128
    flat = jnp.pad(flat, (0, chunk * peers - flat.shape[0]))
    pieces = flat.reshape(peers, chunk // 128, 128)
    arrived = lax.all_to_all(pieces, "atoms", 0, 0, tiled=True)
    if riders is not None:
        arrived, riders = lax.optimization_barrier((arrived, riders))
    owned = jnp.sum(arrived, axis=0, keepdims=True)
    if exact is not None:
        owner, slot = divmod(exact, chunk)
        rest = owned - owned.astype(jnp.bfloat16).astype(jnp.float32)
        here = lax.axis_index("atoms") == owner
        spare = (slot + 1) // 128, (slot + 1) % 128
        row = lax.broadcasted_iota(jnp.int32, owned.shape, 1)
        lane = lax.broadcasted_iota(jnp.int32, owned.shape, 2)
        target = here & (row == spare[0]) & (lane == spare[1])
        owned = jnp.where(target, rest[0, slot // 128, slot % 128], owned).astype(jnp.bfloat16)
    spread = lax.all_to_all(jnp.broadcast_to(owned, pieces.shape), "atoms", 0, 0, tiled=True)
    total = spread.reshape(-1)[: x.size].reshape(x.shape).astype(jnp.float32)
    return total if riders is None else (total, riders)


def feature_map(values):
    return jax.nn.elu(values) + 1.0


def message_pass(atom_rows, tile_pair, tile_block):
    tile_size = tile_block.shape[-1]
    local_rows, half_width = atom_rows.shape
    block_count = local_rows // tile_size
    reach_blocks = max(block_count // 2, 1)
    padded = extended(atom_rows, (("atoms", 0),), reach_blocks * tile_size)
    blocks = padded.reshape(block_count + 2 * reach_blocks, tile_size, half_width)
    first_block = lax.axis_index("atoms") * block_count
    row_ids = tile_pair[0]
    col_ids = tile_pair[1]
    live_tiles = row_ids >= 0
    col_local = jnp.where(live_tiles, col_ids - first_block + reach_blocks, 0)
    row_local = jnp.where(live_tiles, row_ids - first_block, -1)
    panels = jnp.take(blocks, col_local, axis=0)
    selector = row_local[None, :] == jnp.arange(block_count, dtype=jnp.int32)[:, None]
    masked = jnp.where(selector[:, :, None, None], tile_block[None], jnp.zeros_like(tile_block[None]))
    summed = jnp.einsum("btij,tjf->bif", masked, panels, preferred_element_type=jnp.float32)
    return summed.reshape(local_rows, half_width).astype(jnp.bfloat16)


def key_summary(key_rows, value_rows, atom_mask, head_count):
    count_rows = key_rows.shape[0]
    feat_keys = (
        feature_map(key_rows.astype(jnp.float32)).reshape(count_rows, head_count, -1)
        * atom_mask[:, None, None]
    )
    value_f = value_rows.astype(jnp.float32).reshape(count_rows, head_count, -1)
    outer_state = jnp.einsum("nhd,nhe->hde", feat_keys, value_f, precision=HIGHEST)
    return (outer_state, jnp.sum(feat_keys, axis=0))


def read_summary(query_rows, outer_state, key_total, head_count):
    count_rows = query_rows.shape[0]
    feat_query = feature_map(query_rows.astype(jnp.float32)).reshape(count_rows, head_count, -1)
    numerator = jnp.einsum("nhd,hde->nhe", feat_query, outer_state, precision=HIGHEST)
    denominator = jnp.einsum("nhd,hd->nh", feat_query, key_total, precision=HIGHEST)
    return (numerator / denominator[..., None]).reshape(count_rows, -1)


def contrast(unit_rows, peak_rows, label_part, mask_part, peak_start):
    logit_scale = 2.0 / math.sqrt(unit_rows.shape[-1])
    peak_f = peak_rows.astype(jnp.float32)
    logits = logit_scale * jnp.dot(unit_rows, peak_f.T, precision=HIGHEST)
    peak_index = peak_start + jnp.arange(peak_rows.shape[0], dtype=jnp.int32)
    target = (label_part[:, None] == peak_index[None, :]).astype(jnp.float32)
    sign_rows = 2.0 * target - 1.0
    loss_part = jnp.sum(mask_part[:, None] * jax.nn.softplus(-sign_rows * logits)) / PEAKS
    slopes = mask_part[:, None] * (jax.nn.sigmoid(logits) - target) * (1.0 / math.sqrt(PEAKS))
    unit_grad = logit_scale * jnp.dot(slopes, peak_f, precision=HIGHEST)
    return (loss_part, unit_grad)


def embed_backward(unit_rows, unit_grad, embed_scale):
    inner_mean = jnp.mean(unit_grad * unit_rows, axis=-1, keepdims=True)
    return (embed_scale * (unit_grad - unit_rows * inner_mean)).astype(jnp.bfloat16)


def shards(
    atoms_in,
    tile_ids,
    tile_vals,
    seq_lens,
    pair_labels,
    peak_embed,
    norm_gain,
    w_query,
    w_key,
    w_value,
    w_out,
    w_proj,
):
    atom_rows = atoms_in[0]
    local_rows = atom_rows.shape[0]
    gathered = message_pass(atom_rows, tile_ids[0], tile_vals[0])
    hidden_one = (atom_rows.astype(jnp.float32) + gathered.astype(jnp.float32)).astype(jnp.bfloat16)
    atom_base = lax.axis_index("atoms") * local_rows
    length_one = seq_lens[0]
    label_row = pair_labels[0]
    peak_part = peak_embed[0]
    hidden_f = hidden_one.astype(jnp.float32)
    square_part = jnp.sum(hidden_f * hidden_f, axis=-1)
    square_sum = square_part + swap_sec(square_part)
    row_scale = lax.rsqrt(square_sum[:, None] / D + EPSILON)
    normed = (hidden_f * row_scale * norm_gain.astype(jnp.float32)).astype(jnp.bfloat16)
    head_cols = w_query.shape[1]
    sec = lax.axis_index("sec")
    width = normed.shape[1]
    other_rows = swap_sec(normed)
    out_mine = lax.dynamic_slice_in_dim(w_out, sec * width, width, axis=1)
    out_sent = lax.dynamic_slice_in_dim(w_out, (1 - sec) * width, width, axis=1)
    partner = (swap_sec(peak_part), swap_sec(out_sent))

    def project(weight):
        halves = weight.reshape(2, width, weight.shape[1])
        mine = jnp.dot(normed, halves[sec], preferred_element_type=jnp.float32)
        return mine + jnp.dot(other_rows, halves[1 - sec], preferred_element_type=jnp.float32)

    query_f, key_f, value_f = tuple((project(weight) for weight in (w_query, w_key, w_value)))
    head_count = head_cols // HEAD_DIM
    atom_mask = (atom_base + jnp.arange(local_rows, dtype=jnp.int32) < length_one).astype(
        jnp.float32
    )
    outer_state, key_total = key_summary(
        key_f.astype(jnp.bfloat16), value_f.astype(jnp.bfloat16), atom_mask, head_count
    )
    state_rows = jnp.concatenate([outer_state, key_total[:, None, :]], axis=1)
    packed, partner = sum_atoms(state_rows, riders=partner)
    peak_all = join_sec(peak_part, partner[0], sec, 0)
    out_rows = join_sec(out_mine, partner[1], sec, 0)
    outer_state, key_total = packed[:, :HEAD_DIM, :], packed[:, HEAD_DIM, :]
    attended = read_summary(query_f.astype(jnp.bfloat16), outer_state, key_total, head_count)
    attended_all = join_sec(attended, swap_sec(attended), sec, 1)
    out_sum = jnp.sum(attended_all * attended_all, axis=-1)
    attended_n = (attended_all * lax.rsqrt(out_sum[:, None] / (HEADS * HEAD_DIM) + EPSILON)).astype(
        jnp.bfloat16
    )
    branch = jnp.dot(attended_n, out_rows, preferred_element_type=jnp.float32)
    hidden_two = (hidden_f + branch).astype(jnp.bfloat16)
    embedded = sum_sec(jnp.dot(hidden_two, w_proj, preferred_element_type=jnp.float32))
    embed_scale = lax.rsqrt(jnp.mean(embedded * embedded, axis=-1, keepdims=True) + EPSILON)
    unit_rows = embedded * embed_scale
    loss_part, unit_grad = contrast(unit_rows, peak_all, label_row, atom_mask, 0)
    embed_grad = embed_backward(unit_rows, unit_grad, embed_scale)
    proj_part = jnp.einsum("nd,ne->de", hidden_two, embed_grad, preferred_element_type=jnp.float32)
    zero = jnp.zeros((1,), jnp.float32)
    payload = jnp.concatenate([proj_part.reshape(-1), loss_part.reshape(1), zero])
    packed = sum_atoms(payload, exact=proj_part.size)
    proj_total = packed[: proj_part.size].reshape(proj_part.shape)
    loss_sum = packed[proj_part.size] + packed[proj_part.size + 1]
    loss_total = loss_sum / (local_rows * lax.axis_size("atoms"))
    return (hidden_two[None], loss_total.reshape(1), proj_total[None])


def solution(mesh):
    return jax.shard_map(
        shards,
        mesh=mesh,
        in_specs=(
            P("batch", "atoms", "sec"),
            P("batch", None, "atoms"),
            P("batch", "atoms", None, None),
            P("batch"),
            P("batch", "atoms"),
            P("batch", "sec", None),
            P("sec"),
            P(None, "sec"),
            P(None, "sec"),
            P(None, "sec"),
            P("sec", None),
            P("sec", None),
        ),
        out_specs=(P("batch", "atoms", "sec"), P("batch"), P("batch", "sec", None)),
        check_vma=False,
    )
```
